512 devices in a mesh: row: 32 (over x, z_hi, core), col: 16 (over z_lo, y).
Axes of the slice: x: 4, y: 4, z: 16 (z_hi: 4, z_lo: 4; z = z_hi * 4 + z_lo), core: 2. Of those that a mesh axis runs over, the one named last changes fastest.
Arguments:
- images: bfloat16 [32, 128, 128, 256], P('row', 'col'), may hold values from -6 to 6
- weight: bfloat16 [3, 3, 256, 256], P(None, None, None, 'col'), may hold values from -0.125 to 0.125
- norm_gain: float32 [256], replicated, may hold values from 0.5 to 1.5
- cotangent: bfloat16 [32, 128, 128, 256], P('row', 'col'), may hold values from -6 to 6
Outputs:
- features: bfloat16 [32, 128, 128, 256], P('row', 'col')
- input_grad: bfloat16 [32, 128, 128, 256], P('row', 'col')
- weight_grad: float32 [3, 3, 256, 256], P(None, None, None, 'col')
The draws below stay inside these ranges and needn't reach their ends.
All inputs are finite; a program needn't handle non-finite values.
Results may differ from the reference program's by a relative error of at most 0.013.
Values may be sent and summed in bfloat16 or wider, within the bound.
No kernel may reach another device: no remote copies, remote signals or barrier semaphores. Data moves between devices by JAX's collectives and lax.ppermute only.
A program may use at most 64 MiB of HBM per device.

```python
import math
import jax
import jax.numpy as jnp
from jax import lax

CIN = 256
COUT = 256
W = 128
IMGS = 32
H = 128
PIXELS = 524288


def raised(array, own_key, source, target, parts, factor):
    def block_of(axis_at):
        return (jnp.arange(array.shape[axis_at]) // (array.shape[axis_at] // parts)).reshape((-1,) + (1,) * (array.ndim - 1 - axis_at))

    first = jax.random.permutation(own_key, parts)[block_of(target)]
    far = (block_of(target) + parts // 2) % parts
    return jnp.where((block_of(source) == first) | (block_of(source) == far), factor * array, array)


def level_of(stream_key, shape, cuts, least, high):
    loudness = 1.0
    for position, parts in cuts:
        steps = jax.random.uniform(jax.random.fold_in(jax.random.fold_in(stream_key, 6), position), (parts,), jnp.float32, least / len(cuts), high / len(cuts))
        loudness = loudness * jnp.repeat(jnp.exp(steps), shape[position] // parts).reshape((-1,) + (1,) * (len(shape) - 1 - position))
    return loudness


def scatter_about(key, dims, deviation, reach, cuts=(), held_as=jnp.bfloat16):
    values = jax.random.normal(key, dims, jnp.float32) * deviation
    if len(cuts) > 0:
        values = level_of(key, dims, cuts, -0.22, 0.18) * values
    return jnp.clip(values, min=-reach, max=reach).astype(held_as)


def noise_with(stream_key, extent, scale, limit, cuts, heavy, dtype=jnp.bfloat16):
    array = scale * jax.random.normal(stream_key, extent, jnp.float32)
    if cuts:
        array = array * level_of(stream_key, extent, cuts, -0.22, 0.18)
    return jnp.clip(raised(array, jax.random.fold_in(stream_key, 3), *heavy), -limit, limit).astype(dtype)


def setup_inputs(seed: int = 0) -> dict:
    key_list = jax.random.split(jax.random.key(seed), 5)
    return {
        "images": scatter_about(key_list[0], (IMGS, H, W, CIN), 1.0, 6.0, ((0, 32), (1, 16))),
        "weight": scatter_about(key_list[1], (3, 3, CIN, COUT), (9 * CIN) ** -0.5, 0.125, ((3, 16),)),
        "norm_gain": jnp.clip(1.0 + 0.1 * jax.random.normal(key_list[2], (COUT,), jnp.float32), 0.5, 1.5),
        "cotangent": noise_with(key_list[3], (IMGS, H, W, COUT), 1.0, 6.0, ((0, 32), (1, 16)), (1, 3, 16, 2.0)),
    }


epsilon = 1e-06
root_half = 0.7071067811865476
norm_const = 0.3989422804014327

def norm_act(conv_out, upper, norm_gain):
    mean_val = lax.optimization_barrier(jnp.mean(conv_out, axis=-1, keepdims=True))
    centred = conv_out - mean_val
    variance = lax.optimization_barrier(jnp.mean(centred * centred, axis=-1, keepdims=True))
    inv_std = lax.rsqrt(variance + epsilon)
    unit = centred * inv_std
    normed = unit * norm_gain
    cdf_val = 0.5 * (1.0 + lax.erf(normed * root_half))
    density = jnp.exp(-0.5 * normed * normed) * norm_const
    outputs = (normed * cdf_val).astype(jnp.bfloat16)
    upstream = upper.astype(jnp.float32) * (cdf_val + normed * density) * norm_gain
    mean_up = lax.optimization_barrier(jnp.mean(upstream, axis=-1, keepdims=True))
    mean_cross = lax.optimization_barrier(jnp.mean(upstream * unit, axis=-1, keepdims=True))
    grad_pre = inv_std * (upstream - mean_up - unit * mean_cross)
    return (outputs, grad_pre.astype(jnp.bfloat16))

def window(padded, tap_row, tap_col):
    return padded[tap_row:tap_row + H, tap_col:tap_col + W, :].reshape(H * W, padded.shape[-1])

def reference(images, weight, norm_gain, cotangent):

    def one_image(running, sample):
        image_one, cot_one = sample
        padded = jnp.pad(image_one, ((1, 1), (1, 1), (0, 0)))
        conv_out = jnp.zeros((H * W, COUT), jnp.float32)
        for tap_row in range(3):
            for tap_col in range(3):
                conv_out = conv_out + jnp.dot(window(padded, tap_row, tap_col), weight[tap_row, tap_col], preferred_element_type=jnp.float32)
        outputs, grad_pre = norm_act(conv_out, cot_one.reshape(H * W, COUT), norm_gain)
        grad_pad = jnp.pad(grad_pre.reshape(H, W, COUT), ((1, 1), (1, 1), (0, 0)))
        grad_input = jnp.zeros((H * W, CIN), jnp.float32)
        pieces = []
        for tap_row in range(3):
            for tap_col in range(3):
                grad_input = grad_input + lax.dot_general(window(grad_pad, 2 - tap_row, 2 - tap_col), weight[tap_row, tap_col], (((1,), (1,)), ((), ())), preferred_element_type=jnp.float32)
                pieces.append(lax.dot_general(window(padded, tap_row, tap_col), grad_pre, (((0,), (0,)), ((), ())), preferred_element_type=jnp.float32))
        stacked = jnp.stack(pieces).reshape(3, 3, CIN, COUT)
        return (running + stacked, (outputs.reshape(H, W, COUT), grad_input.astype(jnp.bfloat16).reshape(H, W, CIN)))
    running, results = lax.scan(one_image, jnp.zeros((3, 3, CIN, COUT), jnp.float32), (images, cotangent))
    features, input_grad = results
    weight_grad = running * (1.0 / math.sqrt(PIXELS))
    return (features, input_grad, weight_grad)
```

```python
import math

import jax
import jax.numpy as jnp
from jax import lax
from jax.sharding import PartitionSpec as P

epsilon = 1e-06
root_half = 0.7071067811865476
norm_const = 0.3989422804014327


def padded_2(value, sides, width):
    for axis, dim in sides:
        peers, length = (lax.axis_size(axis), value.shape[dim])
        up = [(i, (i + 1) % peers) for i in range(peers - 1)]
        down = [(j, i) for i, j in up]
        last = lax.slice_in_dim(value, length - width, length, axis=dim)
        initial = lax.slice_in_dim(value, 0, width, axis=dim)
        before = lax.ppermute(last, axis, up)
        after = lax.ppermute(initial, axis, down)
        value = jnp.concatenate([before, value, after], axis=dim)
    return value


def norm_act(conv_out, upper, norm_gain):
    mean_val = jnp.mean(conv_out, axis=-1, keepdims=True)
    centred = conv_out - mean_val
    variance = jnp.mean(centred * centred, axis=-1, keepdims=True)
    inv_std = lax.rsqrt(variance + epsilon)
    unit = centred * inv_std
    normed = unit * norm_gain
    cdf_val = 0.5 * (1.0 + lax.erf(normed * root_half))
    density = jnp.exp(-0.5 * normed * normed) * norm_const
    outputs = (normed * cdf_val).astype(jnp.bfloat16)
    upstream = upper.astype(jnp.float32) * (cdf_val + normed * density) * norm_gain
    mean_up = jnp.mean(upstream, axis=-1, keepdims=True)
    mean_cross = jnp.mean(upstream * unit, axis=-1, keepdims=True)
    grad_pre = inv_std * (upstream - mean_up - unit * mean_cross)
    return (outputs, grad_pre.astype(jnp.bfloat16))


def window(padded, tap_row, tap_col, tile_rows, tile_cols):
    return padded[:, tap_row : tap_row + tile_rows, tap_col : tap_col + tile_cols, :].reshape(
        -1, padded.shape[-1]
    )


def on_device(images, weight, norm_gain, cotangent):
    img_count, tile_rows, tile_cols, in_chan = images.shape
    whole_kernel = lax.all_gather(weight, "col", axis=3, tiled=True)
    out_chan = whole_kernel.shape[3]
    rimmed = padded_2(images, (("col", 1),), 1)
    padded = jnp.pad(rimmed, ((0, 0), (0, 0), (1, 1), (0, 0)))
    conv_out = jnp.zeros((img_count * tile_rows * tile_cols, out_chan), jnp.float32)
    for tap_row in range(3):
        for tap_col in range(3):
            conv_out = conv_out + jnp.dot(
                window(padded, tap_row, tap_col, tile_rows, tile_cols),
                whole_kernel[tap_row, tap_col],
                preferred_element_type=jnp.float32,
            )
    outputs, grad_pre = norm_act(conv_out, cotangent.reshape(-1, out_chan), norm_gain)
    grad_grid = grad_pre.reshape(img_count, tile_rows, tile_cols, out_chan)
    grad_rimmed = padded_2(grad_grid, (("col", 1),), 1)
    grad_pad = jnp.pad(grad_rimmed, ((0, 0), (0, 0), (1, 1), (0, 0)))
    grad_input = jnp.zeros((img_count * tile_rows * tile_cols, in_chan), jnp.float32)
    pieces = []
    for tap_row in range(3):
        for tap_col in range(3):
            grad_input = grad_input + lax.dot_general(
                window(grad_pad, 2 - tap_row, 2 - tap_col, tile_rows, tile_cols),
                whole_kernel[tap_row, tap_col],
                (((1,), (1,)), ((), ())),
                preferred_element_type=jnp.float32,
            )
            pieces.append(
                lax.dot_general(
                    window(padded, tap_row, tap_col, tile_rows, tile_cols),
                    grad_pre,
                    (((0,), (0,)), ((), ())),
                    preferred_element_type=jnp.float32,
                )
            )
    partial_value = jnp.stack(pieces).reshape(3, 3, in_chan, out_chan)
    col_sum = lax.psum_scatter(partial_value, "col", scatter_dimension=3, tiled=True)
    own_share = lax.psum(col_sum, "row")
    pixels = img_count * lax.axis_size("row") * tile_rows * lax.axis_size("col") * tile_cols
    weight_grad = own_share * (1.0 / math.sqrt(pixels))
    features = outputs.reshape(img_count, tile_rows, tile_cols, out_chan)
    input_grad = grad_input.astype(jnp.bfloat16).reshape(img_count, tile_rows, tile_cols, in_chan)
    return (features, input_grad, weight_grad)


def solution(mesh):
    placed = (
        P("row", "col", None, None),
        P(None, None, None, "col"),
        P(),
        P("row", "col", None, None),
    )
    return jax.shard_map(
        on_device,
        mesh=mesh,
        in_specs=placed,
        out_specs=(
            P("row", "col", None, None),
            P("row", "col", None, None),
            P(None, None, None, "col"),
        ),
        check_vma=False,
    )
```

```python
import math

import jax
import jax.numpy as jnp
from jax import lax
from jax.sharding import PartitionSpec as P

epsilon = 1e-06
root_half = 0.7071067811865476
norm_const = 0.3989422804014327


def padded_2(value, sides, width):
    for axis, dim in sides:
        peers, length = (lax.axis_size(axis), value.shape[dim])
        up = [(i, (i + 1) % peers) for i in range(peers - 1)]
        down = [(j, i) for i, j in up]
        last = lax.slice_in_dim(value, length - width, length, axis=dim)
        initial = lax.slice_in_dim(value, 0, width, axis=dim)
        before = lax.ppermute(last, axis, up)
        after = lax.ppermute(initial, axis, down)
        value = jnp.concatenate([before, value, after], axis=dim)
    return value


def exchange(value, axis, bit):
    peers = lax.axis_size(axis)
    pairs = [(i, i ^ (1 << bit)) for i in range(peers)]
    return lax.ppermute(value, axis, pairs)


def gather_chunks(value, axis):
    peers, me = lax.axis_size(axis), lax.axis_index(axis)
    held = value[None]
    for bit in range(peers.bit_length() - 1):
        other = exchange(held, axis, bit)
        upper = (me >> bit) & 1
        held = jnp.where(upper == 0, jnp.concatenate([held, other]), jnp.concatenate([other, held]))
    return held


def scatter_sum(value, axis):
    peers, me = lax.axis_size(axis), lax.axis_index(axis)
    held = value
    for bit in reversed(range(peers.bit_length() - 1)):
        half = held.shape[0] // 2
        low, high = held[:half], held[half:]
        upper = ((me >> bit) & 1) == 1
        keep = jnp.where(upper, high, low)
        send = jnp.where(upper, low, high)
        held = keep + exchange(send, axis, bit)
    return held


def total_sum(value, axis):
    peers = lax.axis_size(axis)
    for bit in range(peers.bit_length() - 1):
        value = value + exchange(value, axis, bit)
    return value


def norm_act(conv_out, upper, norm_gain):
    mean_val = jnp.mean(conv_out, axis=-1, keepdims=True)
    centred = conv_out - mean_val
    variance = jnp.mean(centred * centred, axis=-1, keepdims=True)
    inv_std = lax.rsqrt(variance + epsilon)
    unit = centred * inv_std
    normed = unit * norm_gain
    cdf_val = 0.5 * (1.0 + lax.erf(normed * root_half))
    density = jnp.exp(-0.5 * normed * normed) * norm_const
    outputs = (normed * cdf_val).astype(jnp.bfloat16)
    upstream = upper.astype(jnp.float32) * (cdf_val + normed * density) * norm_gain
    mean_up = jnp.mean(upstream, axis=-1, keepdims=True)
    mean_cross = jnp.mean(upstream * unit, axis=-1, keepdims=True)
    grad_pre = inv_std * (upstream - mean_up - unit * mean_cross)
    return (outputs, grad_pre.astype(jnp.bfloat16))


def window(padded, tap_row, tap_col, tile_rows, tile_cols):
    return padded[:, tap_row : tap_row + tile_rows, tap_col : tap_col + tile_cols, :].reshape(
        -1, padded.shape[-1]
    )


def on_device(images, weight, norm_gain, cotangent):
    img_count, tile_rows, tile_cols, in_chan = images.shape
    taps, share = 9 * in_chan, weight.shape[3]
    local_t = weight.reshape(taps, share).T
    kernel_t = gather_chunks(local_t, "col").reshape(-1, taps)
    out_chan = kernel_t.shape[0]
    whole_kernel = kernel_t.T.reshape(3, 3, in_chan, out_chan)
    rimmed = padded_2(images, (("col", 1),), 1)
    padded = jnp.pad(rimmed, ((0, 0), (0, 0), (1, 1), (0, 0)))
    conv_out = jnp.zeros((img_count * tile_rows * tile_cols, out_chan), jnp.float32)
    for tap_row in range(3):
        for tap_col in range(3):
            conv_out = conv_out + jnp.dot(
                window(padded, tap_row, tap_col, tile_rows, tile_cols),
                whole_kernel[tap_row, tap_col],
                preferred_element_type=jnp.float32,
            )
    outputs, grad_pre = norm_act(conv_out, cotangent.reshape(-1, out_chan), norm_gain)
    grad_grid = grad_pre.reshape(img_count, tile_rows, tile_cols, out_chan)
    grad_rimmed = padded_2(grad_grid, (("col", 1),), 1)
    grad_pad = jnp.pad(grad_rimmed, ((0, 0), (0, 0), (1, 1), (0, 0)))
    grad_input = jnp.zeros((img_count * tile_rows * tile_cols, in_chan), jnp.float32)
    pieces = []
    for tap_row in range(3):
        for tap_col in range(3):
            grad_input = grad_input + lax.dot_general(
                window(grad_pad, 2 - tap_row, 2 - tap_col, tile_rows, tile_cols),
                whole_kernel[tap_row, tap_col],
                (((1,), (1,)), ((), ())),
                preferred_element_type=jnp.float32,
            )
            pieces.append(
                lax.dot_general(
                    grad_pre,
                    window(padded, tap_row, tap_col, tile_rows, tile_cols),
                    (((0,), (0,)), ((), ())),
                    preferred_element_type=jnp.float32,
                )
            )
    partial_value = jnp.stack(pieces, axis=1).reshape(out_chan, taps)
    col_sum = scatter_sum(partial_value, "col")
    own_share = total_sum(col_sum, "row")
    pixels = img_count * lax.axis_size("row") * tile_rows * lax.axis_size("col") * tile_cols
    weight_grad = (own_share * (1.0 / math.sqrt(pixels))).T.reshape(3, 3, in_chan, share)
    features = outputs.reshape(img_count, tile_rows, tile_cols, out_chan)
    input_grad = grad_input.astype(jnp.bfloat16).reshape(img_count, tile_rows, tile_cols, in_chan)
    return (features, input_grad, weight_grad)


def solution(mesh):
    placed = (
        P("row", "col", None, None),
        P(None, None, None, "col"),
        P(),
        P("row", "col", None, None),
    )
    return jax.shard_map(
        on_device,
        mesh=mesh,
        in_specs=placed,
        out_specs=(
            P("row", "col", None, None),
            P("row", "col", None, None),
            P(None, None, None, "col"),
        ),
        check_vma=False,
    )
```

```python
import math

import jax
import jax.numpy as jnp
from jax import lax
from jax.sharding import PartitionSpec as P

epsilon = 1e-06
root_half = 0.7071067811865476
norm_const = 0.3989422804014327


def padded_2(value, sides, width):
    for axis, dim in sides:
        peers, length = (lax.axis_size(axis), value.shape[dim])
        up = [(i, (i + 1) % peers) for i in range(peers - 1)]
        down = [(j, i) for i, j in up]
        last = lax.slice_in_dim(value, length - width, length, axis=dim)
        initial = lax.slice_in_dim(value, 0, width, axis=dim)
        before = lax.ppermute(last, axis, up)
        after = lax.ppermute(initial, axis, down)
        value = jnp.concatenate([before, value, after], axis=dim)
    return value


def exchange(value, axis, bit):
    peers = lax.axis_size(axis)
    pairs = [(i, i ^ (1 << bit)) for i in range(peers)]
    return lax.ppermute(value, axis, pairs)


def gather_chunks(value, axis):
    peers = lax.axis_size(axis)
    copies = jnp.broadcast_to(value[None], (peers,) + value.shape)
    return lax.all_to_all(copies, axis, 0, 0, tiled=False)


def scatter_sum(value, axis):
    peers = lax.axis_size(axis)
    blocks = value.reshape((peers, value.shape[0] // peers) + value.shape[1:])
    return lax.all_to_all(blocks, axis, 0, 0, tiled=False).sum(0)


def split_pair(value, upper, dim):
    low, high = jnp.split(value, 2, axis=dim)
    return jnp.where(upper, high, low), jnp.where(upper, low, high)


def join_pair(value, other, upper, dim):
    return jnp.where(upper, jnp.concatenate([other, value], dim), jnp.concatenate([value, other], dim))


def halve_sum(value, axis, bits, dim):
    me = lax.axis_index(axis)
    for bit in bits:
        keep, send = split_pair(value, ((me >> bit) & 1) == 1, dim)
        value = keep + exchange(send, axis, bit)
    return value


def double_sum(value, axis, bits):
    for bit in bits:
        value = value + exchange(value, axis, bit)
    return value


def double_join(value, axis, bits, dim):
    me = lax.axis_index(axis)
    for bit in bits:
        value = join_pair(value, exchange(value, axis, bit), ((me >> bit) & 1) == 1, dim)
    return value


def norm_act(conv_out, upper, norm_gain):
    mean_val = jnp.mean(conv_out, axis=-1, keepdims=True)
    centred = conv_out - mean_val
    variance = jnp.mean(centred * centred, axis=-1, keepdims=True)
    inv_std = lax.rsqrt(variance + epsilon)
    unit = centred * inv_std
    normed = unit * norm_gain
    cdf_val = 0.5 * (1.0 + lax.erf(normed * root_half))
    density = jnp.exp(-0.5 * normed * normed) * norm_const
    outputs = (normed * cdf_val).astype(jnp.bfloat16)
    upstream = upper.astype(jnp.float32) * (cdf_val + normed * density) * norm_gain
    mean_up = jnp.mean(upstream, axis=-1, keepdims=True)
    mean_cross = jnp.mean(upstream * unit, axis=-1, keepdims=True)
    grad_pre = inv_std * (upstream - mean_up - unit * mean_cross)
    return (outputs, grad_pre.astype(jnp.bfloat16))


def window(padded, tap_row, tap_col, tile_rows, tile_cols):
    return padded[:, tap_row : tap_row + tile_rows, tap_col : tap_col + tile_cols, :].reshape(
        -1, padded.shape[-1]
    )


def on_device(images, weight, norm_gain, cotangent):
    img_count, tile_rows, tile_cols, in_chan = images.shape
    taps, share = 9 * in_chan, weight.shape[3]
    local_t = weight.reshape(taps, share).T
    core_bit = [0]
    half_t, _ = split_pair(local_t, (lax.axis_index("row") & 1) == 1, 1)
    kernel_t = double_join(gather_chunks(half_t, "col"), "row", core_bit, 2).reshape(-1, taps)
    out_chan = kernel_t.shape[0]
    whole_kernel = kernel_t.T.reshape(3, 3, in_chan, out_chan)
    rimmed = padded_2(images, (("col", 1),), 1)
    padded = jnp.pad(rimmed, ((0, 0), (0, 0), (1, 1), (0, 0)))
    conv_out = jnp.zeros((img_count * tile_rows * tile_cols, out_chan), jnp.float32)
    for tap_row in range(3):
        for tap_col in range(3):
            conv_out = conv_out + jnp.dot(
                window(padded, tap_row, tap_col, tile_rows, tile_cols),
                whole_kernel[tap_row, tap_col],
                preferred_element_type=jnp.float32,
            )
    outputs, grad_pre = norm_act(conv_out, cotangent.reshape(-1, out_chan), norm_gain)
    grad_grid = grad_pre.reshape(img_count, tile_rows, tile_cols, out_chan)
    grad_rimmed = padded_2(grad_grid, (("col", 1),), 1)
    grad_pad = jnp.pad(grad_rimmed, ((0, 0), (0, 0), (1, 1), (0, 0)))
    grad_input = jnp.zeros((img_count * tile_rows * tile_cols, in_chan), jnp.float32)
    pieces = []
    for tap_row in range(3):
        for tap_col in range(3):
            grad_input = grad_input + lax.dot_general(
                window(grad_pad, 2 - tap_row, 2 - tap_col, tile_rows, tile_cols),
                whole_kernel[tap_row, tap_col],
                (((1,), (1,)), ((), ())),
                preferred_element_type=jnp.float32,
            )
            pieces.append(
                lax.dot_general(
                    grad_pre,
                    window(padded, tap_row, tap_col, tile_rows, tile_cols),
                    (((0,), (0,)), ((), ())),
                    preferred_element_type=jnp.float32,
                )
            )
    partial_value = jnp.stack(pieces, axis=1).reshape(out_chan, taps)
    core_sum = halve_sum(partial_value, "row", core_bit, 1)
    col_sum = scatter_sum(core_sum, "col")
    x_piece = halve_sum(col_sum, "row", [3, 4], 1)
    row_piece = double_sum(x_piece, "row", [1, 2])
    own_share = double_join(row_piece, "row", [4, 3, 0], 1)
    pixels = img_count * lax.axis_size("row") * tile_rows * lax.axis_size("col") * tile_cols
    weight_grad = (own_share * (1.0 / math.sqrt(pixels))).T.reshape(3, 3, in_chan, share)
    features = outputs.reshape(img_count, tile_rows, tile_cols, out_chan)
    input_grad = grad_input.astype(jnp.bfloat16).reshape(img_count, tile_rows, tile_cols, in_chan)
    return (features, input_grad, weight_grad)


def solution(mesh):
    placed = (
        P("row", "col", None, None),
        P(None, None, None, "col"),
        P(),
        P("row", "col", None, None),
    )
    return jax.shard_map(
        on_device,
        mesh=mesh,
        in_specs=placed,
        out_specs=(
            P("row", "col", None, None),
            P("row", "col", None, None),
            P(None, None, None, "col"),
        ),
        check_vma=False,
    )
```

```python
import itertools
import math

import jax
import jax.numpy as jnp
from jax import lax
from jax.sharding import PartitionSpec as P

epsilon = 1e-06
root_half = 0.7071067811865476
norm_const = 0.3989422804014327


def padded_2(value, sides, width):
    for axis, dim in sides:
        peers, length = (lax.axis_size(axis), value.shape[dim])
        up = [(i, (i + 1) % peers) for i in range(peers - 1)]
        down = [(j, i) for i, j in up]
        last = lax.slice_in_dim(value, length - width, length, axis=dim)
        initial = lax.slice_in_dim(value, 0, width, axis=dim)
        before = lax.ppermute(last, axis, up)
        after = lax.ppermute(initial, axis, down)
        value = jnp.concatenate([before, value, after], axis=dim)
    return value


def exchange(value, axis, bit):
    peers = lax.axis_size(axis)
    pairs = [(i, i ^ (1 << bit)) for i in range(peers)]
    return lax.ppermute(value, axis, pairs)


def gather_chunks(value, axis):
    peers = lax.axis_size(axis)
    copies = jnp.broadcast_to(value[None], (peers,) + value.shape)
    return lax.all_to_all(copies, axis, 0, 0, tiled=False)


def scatter_sum(value, axis):
    peers = lax.axis_size(axis)
    blocks = value.reshape((peers, value.shape[0] // peers) + value.shape[1:])
    return lax.all_to_all(blocks, axis, 0, 0, tiled=False).sum(0)


def split_pair(value, upper, dim):
    low, high = jnp.split(value, 2, axis=dim)
    return jnp.where(upper, high, low), jnp.where(upper, low, high)


def halve_sum(value, axis, bits, dim):
    me = lax.axis_index(axis)
    for bit in bits:
        keep, send = split_pair(value, ((me >> bit) & 1) == 1, dim)
        value = keep + exchange(send, axis, bit)
    return value


def field_shift(peers, low, size, step):
    mask = (size - 1) << low
    return [(i, (i & ~mask) | (((((i >> low) % size) + step) % size) << low)) for i in range(peers)]


def field_of(axis, low, size):
    return (lax.axis_index(axis) >> low) % size


def scatter_field(value, axis, low, size, dim):
    peers, me = lax.axis_size(axis), field_of(axis, low, size)
    pieces = jnp.stack(jnp.split(value, size, axis=dim))
    got = [jnp.take(pieces, me, axis=0)]
    for step in range(1, size):
        sent = jnp.take(pieces, (me + step) % size, axis=0)
        got.append(lax.ppermute(sent, axis, field_shift(peers, low, size, step)))
    got = jnp.stack(got)
    return jnp.take(got, (me - jnp.arange(size)) % size, axis=0).sum(0)


def sum_field(value, axis, low, size):
    peers, me = lax.axis_size(axis), field_of(axis, low, size)
    got = [value] + [lax.ppermute(value, axis, field_shift(peers, low, size, step)) for step in range(1, size)]
    got = jnp.stack(got)
    return jnp.take(got, (me - jnp.arange(size)) % size, axis=0).sum(0)


def gather_fields(value, axis, fields):
    peers = lax.axis_size(axis)
    shape = tuple(size for _, size in fields)
    held = jnp.zeros(shape + value.shape, value.dtype)
    for offsets in itertools.product(*[range(size) for _, size in fields]):
        target = list(range(peers))
        for (low, size), step in zip(fields, offsets):
            moved = dict(field_shift(peers, low, size, step))
            target = [moved[j] for j in target]
        source = tuple((field_of(axis, low, size) - step) % size for (low, size), step in zip(fields, offsets))
        piece = lax.ppermute(value, axis, list(enumerate(target))) if any(offsets) else value
        held = held.at[source].set(piece)
    return held


def norm_act(conv_out, upper, norm_gain):
    mean_val = jnp.mean(conv_out, axis=-1, keepdims=True)
    centred = conv_out - mean_val
    variance = jnp.mean(centred * centred, axis=-1, keepdims=True)
    inv_std = lax.rsqrt(variance + epsilon)
    unit = centred * inv_std
    normed = unit * norm_gain
    cdf_val = 0.5 * (1.0 + lax.erf(normed * root_half))
    density = jnp.exp(-0.5 * normed * normed) * norm_const
    outputs = (normed * cdf_val).astype(jnp.bfloat16)
    upstream = upper.astype(jnp.float32) * (cdf_val + normed * density) * norm_gain
    mean_up = jnp.mean(upstream, axis=-1, keepdims=True)
    mean_cross = jnp.mean(upstream * unit, axis=-1, keepdims=True)
    grad_pre = inv_std * (upstream - mean_up - unit * mean_cross)
    return (outputs, grad_pre.astype(jnp.bfloat16))


def window(padded, tap_row, tap_col, tile_rows, tile_cols):
    return padded[:, tap_row : tap_row + tile_rows, tap_col : tap_col + tile_cols, :].reshape(
        -1, padded.shape[-1]
    )


def on_device(images, weight, norm_gain, cotangent):
    img_count, tile_rows, tile_cols, in_chan = images.shape
    taps, share = 9 * in_chan, weight.shape[3]
    local_t = weight.reshape(taps, share).T
    core_bit = [0]
    half_t, _ = split_pair(local_t, (lax.axis_index("row") & 1) == 1, 1)
    halves = gather_fields(gather_chunks(half_t, "col"), "row", [(0, 2)])
    kernel_t = jnp.concatenate([halves[0], halves[1]], 2).reshape(-1, taps)
    out_chan = kernel_t.shape[0]
    whole_kernel = kernel_t.T.reshape(3, 3, in_chan, out_chan)
    rimmed = padded_2(images, (("col", 1),), 1)
    padded = jnp.pad(rimmed, ((0, 0), (0, 0), (1, 1), (0, 0)))
    conv_out = jnp.zeros((img_count * tile_rows * tile_cols, out_chan), jnp.float32)
    for tap_row in range(3):
        for tap_col in range(3):
            conv_out = conv_out + jnp.dot(
                window(padded, tap_row, tap_col, tile_rows, tile_cols),
                whole_kernel[tap_row, tap_col],
                preferred_element_type=jnp.float32,
            )
    outputs, grad_pre = norm_act(conv_out, cotangent.reshape(-1, out_chan), norm_gain)
    grad_grid = grad_pre.reshape(img_count, tile_rows, tile_cols, out_chan)
    grad_rimmed = padded_2(grad_grid, (("col", 1),), 1)
    grad_pad = jnp.pad(grad_rimmed, ((0, 0), (0, 0), (1, 1), (0, 0)))
    grad_input = jnp.zeros((img_count * tile_rows * tile_cols, in_chan), jnp.float32)
    pieces = []
    for tap_row in range(3):
        for tap_col in range(3):
            grad_input = grad_input + lax.dot_general(
                window(grad_pad, 2 - tap_row, 2 - tap_col, tile_rows, tile_cols),
                whole_kernel[tap_row, tap_col],
                (((1,), (1,)), ((), ())),
                preferred_element_type=jnp.float32,
            )
            pieces.append(
                lax.dot_general(
                    grad_pre,
                    window(padded, tap_row, tap_col, tile_rows, tile_cols),
                    (((0,), (0,)), ((), ())),
                    preferred_element_type=jnp.float32,
                )
            )
    partial_value = jnp.stack(pieces, axis=1).reshape(out_chan, taps)
    core_sum = halve_sum(partial_value, "row", core_bit, 1)
    col_sum = scatter_sum(core_sum, "col")
    x_piece = scatter_field(col_sum, "row", 3, 4, 1)
    row_piece = sum_field(x_piece, "row", 1, 4)
    pieces = gather_fields(row_piece, "row", [(0, 2), (3, 4)])
    own_share = pieces.transpose(2, 0, 1, 3).reshape(row_piece.shape[0], -1)
    pixels = img_count * lax.axis_size("row") * tile_rows * lax.axis_size("col") * tile_cols
    weight_grad = (own_share * (1.0 / math.sqrt(pixels))).T.reshape(3, 3, in_chan, share)
    features = outputs.reshape(img_count, tile_rows, tile_cols, out_chan)
    input_grad = grad_input.astype(jnp.bfloat16).reshape(img_count, tile_rows, tile_cols, in_chan)
    return (features, input_grad, weight_grad)


def solution(mesh):
    placed = (
        P("row", "col", None, None),
        P(None, None, None, "col"),
        P(),
        P("row", "col", None, None),
    )
    return jax.shard_map(
        on_device,
        mesh=mesh,
        in_specs=placed,
        out_specs=(
            P("row", "col", None, None),
            P("row", "col", None, None),
            P(None, None, None, "col"),
        ),
        check_vma=False,
    )
```

```python
import math

import jax
import jax.numpy as jnp
from jax import lax
from jax.sharding import PartitionSpec as P

epsilon = 1e-06
root_half = 0.7071067811865476
norm_const = 0.3989422804014327


def padded_2(value, sides, width):
    for axis, dim in sides:
        peers, length = (lax.axis_size(axis), value.shape[dim])
        up = [(i, (i + 1) % peers) for i in range(peers - 1)]
        down = [(j, i) for i, j in up]
        last = lax.slice_in_dim(value, length - width, length, axis=dim)
        initial = lax.slice_in_dim(value, 0, width, axis=dim)
        before = lax.ppermute(last, axis, up)
        after = lax.ppermute(initial, axis, down)
        value = jnp.concatenate([before, value, after], axis=dim)
    return value


def exchange(value, axis, bit):
    peers = lax.axis_size(axis)
    pairs = [(i, i ^ (1 << bit)) for i in range(peers)]
    return lax.ppermute(value, axis, pairs)


def gather_chunks(value, axis):
    peers = lax.axis_size(axis)
    copies = jnp.broadcast_to(value[None], (peers,) + value.shape)
    return lax.all_to_all(copies, axis, 0, 0, tiled=False)


def scatter_sum(value, axis):
    peers = lax.axis_size(axis)
    blocks = value.reshape((peers, value.shape[0] // peers) + value.shape[1:])
    return lax.all_to_all(blocks, axis, 0, 0, tiled=False).sum(0)


def split_pair(value, upper, dim):
    low, high = jnp.split(value, 2, axis=dim)
    return jnp.where(upper, high, low), jnp.where(upper, low, high)


def join_pair(value, other, upper, dim):
    return jnp.where(upper, jnp.concatenate([other, value], dim), jnp.concatenate([value, other], dim))


def halve_sum(value, axis, bits, dim):
    me = lax.axis_index(axis)
    for bit in bits:
        keep, send = split_pair(value, ((me >> bit) & 1) == 1, dim)
        value = keep + exchange(send, axis, bit)
    return value


def double_sum(value, axis, bits):
    for bit in bits:
        value = value + exchange(value, axis, bit)
    return value


def double_join(value, axis, bits, dim):
    me = lax.axis_index(axis)
    for bit in bits:
        value = join_pair(value, exchange(value, axis, bit), ((me >> bit) & 1) == 1, dim)
    return value


def norm_act(conv_out, upper, norm_gain):
    mean_val = jnp.mean(conv_out, axis=-1, keepdims=True)
    centred = conv_out - mean_val
    variance = jnp.mean(centred * centred, axis=-1, keepdims=True)
    inv_std = lax.rsqrt(variance + epsilon)
    unit = centred * inv_std
    normed = unit * norm_gain
    cdf_val = 0.5 * (1.0 + lax.erf(normed * root_half))
    density = jnp.exp(-0.5 * normed * normed) * norm_const
    outputs = (normed * cdf_val).astype(jnp.bfloat16)
    upstream = upper.astype(jnp.float32) * (cdf_val + normed * density) * norm_gain
    mean_up = jnp.mean(upstream, axis=-1, keepdims=True)
    mean_cross = jnp.mean(upstream * unit, axis=-1, keepdims=True)
    grad_pre = inv_std * (upstream - mean_up - unit * mean_cross)
    return (outputs, grad_pre.astype(jnp.bfloat16))


def window(padded, tap_row, tap_col, tile_rows, tile_cols):
    return padded[:, tap_row : tap_row + tile_rows, tap_col : tap_col + tile_cols, :].reshape(
        -1, padded.shape[-1]
    )


def on_device(images, weight, norm_gain, cotangent):
    img_count, tile_rows, tile_cols, in_chan = images.shape
    taps, share = 9 * in_chan, weight.shape[3]
    local_t = weight.reshape(taps, share).T
    core_bit = [0]
    half_t, _ = split_pair(local_t, (lax.axis_index("row") & 1) == 1, 1)
    kernel_t = double_join(gather_chunks(half_t, "col"), "row", core_bit, 2).reshape(-1, taps)
    out_chan = kernel_t.shape[0]
    whole_kernel = kernel_t.T.reshape(3, 3, in_chan, out_chan)
    rimmed = padded_2(images, (("col", 1),), 1)
    padded = jnp.pad(rimmed, ((0, 0), (0, 0), (1, 1), (0, 0)))
    conv_out = jnp.zeros((img_count * tile_rows * tile_cols, out_chan), jnp.float32)
    for tap_row in range(3):
        for tap_col in range(3):
            conv_out = conv_out + jnp.dot(
                window(padded, tap_row, tap_col, tile_rows, tile_cols),
                whole_kernel[tap_row, tap_col],
                preferred_element_type=jnp.float32,
            )
    outputs, grad_pre = norm_act(conv_out, cotangent.reshape(-1, out_chan), norm_gain)
    grad_grid = grad_pre.reshape(img_count, tile_rows, tile_cols, out_chan)
    grad_rimmed = padded_2(grad_grid, (("col", 1),), 1)
    grad_pad = jnp.pad(grad_rimmed, ((0, 0), (0, 0), (1, 1), (0, 0)))
    grad_input = jnp.zeros((img_count * tile_rows * tile_cols, in_chan), jnp.float32)
    pieces = []
    for tap_row in range(3):
        for tap_col in range(3):
            grad_input = grad_input + lax.dot_general(
                window(grad_pad, 2 - tap_row, 2 - tap_col, tile_rows, tile_cols),
                whole_kernel[tap_row, tap_col],
                (((1,), (1,)), ((), ())),
                preferred_element_type=jnp.float32,
            )
            pieces.append(
                lax.dot_general(
                    grad_pre,
                    window(padded, tap_row, tap_col, tile_rows, tile_cols),
                    (((0,), (0,)), ((), ())),
                    preferred_element_type=jnp.float32,
                )
            )
    partial_value = jnp.stack(pieces, axis=1).reshape(out_chan, taps)
    core_sum = halve_sum(partial_value, "row", core_bit, 1)
    col_sum = scatter_sum(core_sum, "col")
    row_piece = double_sum(col_sum, "row", [3, 4, 1, 2])
    own_share = double_join(row_piece, "row", core_bit, 1)
    pixels = img_count * lax.axis_size("row") * tile_rows * lax.axis_size("col") * tile_cols
    weight_grad = (own_share * (1.0 / math.sqrt(pixels))).T.reshape(3, 3, in_chan, share)
    features = outputs.reshape(img_count, tile_rows, tile_cols, out_chan)
    input_grad = grad_input.astype(jnp.bfloat16).reshape(img_count, tile_rows, tile_cols, in_chan)
    return (features, input_grad, weight_grad)


def solution(mesh):
    placed = (
        P("row", "col", None, None),
        P(None, None, None, "col"),
        P(),
        P("row", "col", None, None),
    )
    return jax.shard_map(
        on_device,
        mesh=mesh,
        in_specs=placed,
        out_specs=(
            P("row", "col", None, None),
            P("row", "col", None, None),
            P(None, None, None, "col"),
        ),
        check_vma=False,
    )
```

```python
import math

import jax
import jax.numpy as jnp
from jax import lax
from jax.sharding import PartitionSpec as P

epsilon = 1e-06
root_half = 0.7071067811865476
norm_const = 0.3989422804014327


def padded_2(value, sides, width):
    for axis, dim in sides:
        peers, length = (lax.axis_size(axis), value.shape[dim])
        up = [(i, (i + 1) % peers) for i in range(peers - 1)]
        down = [(j, i) for i, j in up]
        last = lax.slice_in_dim(value, length - width, length, axis=dim)
        initial = lax.slice_in_dim(value, 0, width, axis=dim)
        before = lax.ppermute(last, axis, up)
        after = lax.ppermute(initial, axis, down)
        value = jnp.concatenate([before, value, after], axis=dim)
    return value


def exchange(value, axis, bit, mask=None):
    peers = lax.axis_size(axis)
    mask = 1 << bit if mask is None else mask
    pairs = [(i, i ^ mask) for i in range(peers)]
    return lax.ppermute(value, axis, pairs)


def gather_chunks(value, axis):
    peers = lax.axis_size(axis)
    copies = jnp.broadcast_to(value[None], (peers,) + value.shape)
    return lax.all_to_all(copies, axis, 0, 0, tiled=False)


def scatter_sum(value, axis):
    peers = lax.axis_size(axis)
    blocks = value.reshape((peers, value.shape[0] // peers) + value.shape[1:])
    return lax.all_to_all(blocks, axis, 0, 0, tiled=False).sum(0)


def split_pair(value, upper, dim):
    low, high = jnp.split(value, 2, axis=dim)
    return jnp.where(upper, high, low), jnp.where(upper, low, high)


def join_pair(value, other, upper, dim):
    return jnp.where(upper, jnp.concatenate([other, value], dim), jnp.concatenate([value, other], dim))


def halve_sum(value, axis, bits, dim):
    me = lax.axis_index(axis)
    for bit in bits:
        keep, send = split_pair(value, ((me >> bit) & 1) == 1, dim)
        value = keep + exchange(send, axis, bit)
    return value


def double_sum(value, axis, masks):
    for mask in masks:
        value = value + exchange(value, axis, 0, mask)
    return value


def double_join(value, axis, bits, dim):
    me = lax.axis_index(axis)
    for bit in bits:
        value = join_pair(value, exchange(value, axis, bit), ((me >> bit) & 1) == 1, dim)
    return value


def norm_act(conv_out, upper, norm_gain):
    mean_val = jnp.mean(conv_out, axis=-1, keepdims=True)
    centred = conv_out - mean_val
    variance = jnp.mean(centred * centred, axis=-1, keepdims=True)
    inv_std = lax.rsqrt(variance + epsilon)
    unit = centred * inv_std
    normed = unit * norm_gain
    cdf_val = 0.5 * (1.0 + lax.erf(normed * root_half))
    density = jnp.exp(-0.5 * normed * normed) * norm_const
    outputs = (normed * cdf_val).astype(jnp.bfloat16)
    upstream = upper.astype(jnp.float32) * (cdf_val + normed * density) * norm_gain
    mean_up = jnp.mean(upstream, axis=-1, keepdims=True)
    mean_cross = jnp.mean(upstream * unit, axis=-1, keepdims=True)
    grad_pre = inv_std * (upstream - mean_up - unit * mean_cross)
    return (outputs, grad_pre.astype(jnp.bfloat16))


def window(padded, tap_row, tap_col, tile_rows, tile_cols):
    return padded[:, tap_row : tap_row + tile_rows, tap_col : tap_col + tile_cols, :].reshape(
        -1, padded.shape[-1]
    )


def on_device(images, weight, norm_gain, cotangent):
    img_count, tile_rows, tile_cols, in_chan = images.shape
    taps, share = 9 * in_chan, weight.shape[3]
    local_t = weight.reshape(taps, share).T
    core_bit = [0]
    half_t, _ = split_pair(local_t, (lax.axis_index("row") & 1) == 1, 1)
    kernel_t = double_join(gather_chunks(half_t, "col"), "row", core_bit, 2).reshape(-1, taps)
    out_chan = kernel_t.shape[0]
    whole_kernel = kernel_t.T.reshape(3, 3, in_chan, out_chan)
    rimmed = padded_2(images, (("col", 1),), 1)
    padded = jnp.pad(rimmed, ((0, 0), (0, 0), (1, 1), (0, 0)))
    conv_out = jnp.zeros((img_count * tile_rows * tile_cols, out_chan), jnp.float32)
    for tap_row in range(3):
        for tap_col in range(3):
            conv_out = conv_out + jnp.dot(
                window(padded, tap_row, tap_col, tile_rows, tile_cols),
                whole_kernel[tap_row, tap_col],
                preferred_element_type=jnp.float32,
            )
    outputs, grad_pre = norm_act(conv_out, cotangent.reshape(-1, out_chan), norm_gain)
    grad_grid = grad_pre.reshape(img_count, tile_rows, tile_cols, out_chan)
    grad_rimmed = padded_2(grad_grid, (("col", 1),), 1)
    grad_pad = jnp.pad(grad_rimmed, ((0, 0), (0, 0), (1, 1), (0, 0)))
    grad_input = jnp.zeros((img_count * tile_rows * tile_cols, in_chan), jnp.float32)
    pieces = []
    for tap_row in range(3):
        for tap_col in range(3):
            grad_input = grad_input + lax.dot_general(
                window(grad_pad, 2 - tap_row, 2 - tap_col, tile_rows, tile_cols),
                whole_kernel[tap_row, tap_col],
                (((1,), (1,)), ((), ())),
                preferred_element_type=jnp.float32,
            )
            pieces.append(
                lax.dot_general(
                    grad_pre,
                    window(padded, tap_row, tap_col, tile_rows, tile_cols),
                    (((0,), (0,)), ((), ())),
                    preferred_element_type=jnp.float32,
                )
            )
    partial_value = jnp.stack(pieces, axis=1).reshape(out_chan, taps)
    core_sum = halve_sum(partial_value, "row", core_bit, 1)
    col_sum = scatter_sum(core_sum, "col")
    row_piece = double_sum(col_sum, "row", [1 << 3, 3 << 3, 1 << 1, 3 << 1])
    own_share = double_join(row_piece, "row", core_bit, 1)
    pixels = img_count * lax.axis_size("row") * tile_rows * lax.axis_size("col") * tile_cols
    weight_grad = (own_share * (1.0 / math.sqrt(pixels))).T.reshape(3, 3, in_chan, share)
    features = outputs.reshape(img_count, tile_rows, tile_cols, out_chan)
    input_grad = grad_input.astype(jnp.bfloat16).reshape(img_count, tile_rows, tile_cols, in_chan)
    return (features, input_grad, weight_grad)


def solution(mesh):
    placed = (
        P("row", "col", None, None),
        P(None, None, None, "col"),
        P(),
        P("row", "col", None, None),
    )
    return jax.shard_map(
        on_device,
        mesh=mesh,
        in_specs=placed,
        out_specs=(
            P("row", "col", None, None),
            P("row", "col", None, None),
            P(None, None, None, "col"),
        ),
        check_vma=False,
    )
```

```python
import math

import jax
import jax.numpy as jnp
from jax import lax
from jax.sharding import PartitionSpec as P

epsilon = 1e-06
root_half = 0.7071067811865476
norm_const = 0.3989422804014327


def padded_2(value, sides, width):
    for axis, dim in sides:
        peers, length = (lax.axis_size(axis), value.shape[dim])
        up = [(i, (i + 1) % peers) for i in range(peers - 1)]
        down = [(j, i) for i, j in up]
        last = lax.slice_in_dim(value, length - width, length, axis=dim)
        initial = lax.slice_in_dim(value, 0, width, axis=dim)
        before = lax.ppermute(last, axis, up)
        after = lax.ppermute(initial, axis, down)
        value = jnp.concatenate([before, value, after], axis=dim)
    return value


def exchange(value, axis, bit, mask=None):
    peers = lax.axis_size(axis)
    mask = 1 << bit if mask is None else mask
    pairs = [(i, i ^ mask) for i in range(peers)]
    return lax.ppermute(value, axis, pairs)


def gather_chunks(value, axis):
    peers = lax.axis_size(axis)
    copies = jnp.broadcast_to(value[None], (peers,) + value.shape)
    return lax.all_to_all(copies, axis, 0, 0, tiled=False)


def scatter_sum(value, axis):
    peers = lax.axis_size(axis)
    blocks = value.reshape((peers, value.shape[0] // peers) + value.shape[1:])
    return lax.all_to_all(blocks, axis, 0, 0, tiled=False).sum(0)


def split_pair(value, upper, dim):
    low, high = jnp.split(value, 2, axis=dim)
    return jnp.where(upper, high, low), jnp.where(upper, low, high)


def join_pair(value, other, upper, dim):
    return jnp.where(upper, jnp.concatenate([other, value], dim), jnp.concatenate([value, other], dim))


def halve_sum(value, axis, bits, dim):
    me = lax.axis_index(axis)
    for bit in bits:
        keep, send = split_pair(value, ((me >> bit) & 1) == 1, dim)
        value = keep + exchange(send, axis, bit)
    return value


def double_sum(value, axis, masks):
    for mask in masks:
        value = value + exchange(value, axis, 0, mask)
    return value


def double_join(value, axis, bits, dim):
    me = lax.axis_index(axis)
    for bit in bits:
        value = join_pair(value, exchange(value, axis, bit), ((me >> bit) & 1) == 1, dim)
    return value


def norm_act(conv_out, upper, norm_gain):
    mean_val = jnp.mean(conv_out, axis=-1, keepdims=True)
    centred = conv_out - mean_val
    variance = jnp.mean(centred * centred, axis=-1, keepdims=True)
    inv_std = lax.rsqrt(variance + epsilon)
    unit = centred * inv_std
    normed = unit * norm_gain
    cdf_val = 0.5 * (1.0 + lax.erf(normed * root_half))
    density = jnp.exp(-0.5 * normed * normed) * norm_const
    outputs = (normed * cdf_val).astype(jnp.bfloat16)
    upstream = upper.astype(jnp.float32) * (cdf_val + normed * density) * norm_gain
    mean_up = jnp.mean(upstream, axis=-1, keepdims=True)
    mean_cross = jnp.mean(upstream * unit, axis=-1, keepdims=True)
    grad_pre = inv_std * (upstream - mean_up - unit * mean_cross)
    return (outputs, grad_pre.astype(jnp.bfloat16))


def window(padded, tap_row, tap_col, tile_rows, tile_cols):
    return padded[:, tap_row : tap_row + tile_rows, tap_col : tap_col + tile_cols, :].reshape(
        -1, padded.shape[-1]
    )


def on_device(images, weight, norm_gain, cotangent):
    img_count, tile_rows, tile_cols, in_chan = images.shape
    taps, share = 9 * in_chan, weight.shape[3]
    local_t = weight.reshape(taps, share).T
    core_bit = [0]
    half_t, _ = split_pair(local_t, (lax.axis_index("row") & 1) == 1, 1)
    kernel_t = double_join(gather_chunks(half_t, "col"), "row", core_bit, 2).reshape(-1, taps)
    out_chan = kernel_t.shape[0]
    whole_kernel = kernel_t.T.reshape(3, 3, in_chan, out_chan)
    rimmed = padded_2(images, (("col", 1),), 1)
    padded = jnp.pad(rimmed, ((0, 0), (0, 0), (1, 1), (0, 0)))
    conv_out = jnp.zeros((img_count * tile_rows * tile_cols, out_chan), jnp.float32)
    for tap_row in range(3):
        for tap_col in range(3):
            conv_out = conv_out + jnp.dot(
                window(padded, tap_row, tap_col, tile_rows, tile_cols),
                whole_kernel[tap_row, tap_col],
                preferred_element_type=jnp.float32,
            )
    outputs, grad_pre = norm_act(conv_out, cotangent.reshape(-1, out_chan), norm_gain)
    grad_grid = grad_pre.reshape(img_count, tile_rows, tile_cols, out_chan)
    grad_rimmed = padded_2(grad_grid, (("col", 1),), 1)
    grad_rimmed, grad_pre = lax.optimization_barrier((grad_rimmed, grad_pre))
    grad_pad = jnp.pad(grad_rimmed, ((0, 0), (0, 0), (1, 1), (0, 0)))
    grad_input = jnp.zeros((img_count * tile_rows * tile_cols, in_chan), jnp.float32)
    pieces = []
    for tap_row in range(3):
        for tap_col in range(3):
            grad_input = grad_input + lax.dot_general(
                window(grad_pad, 2 - tap_row, 2 - tap_col, tile_rows, tile_cols),
                whole_kernel[tap_row, tap_col],
                (((1,), (1,)), ((), ())),
                preferred_element_type=jnp.float32,
            )
            pieces.append(
                lax.dot_general(
                    grad_pre,
                    window(padded, tap_row, tap_col, tile_rows, tile_cols),
                    (((0,), (0,)), ((), ())),
                    preferred_element_type=jnp.float32,
                )
            )
    partial_value = jnp.stack(pieces, axis=1).reshape(out_chan, taps)
    core_sum = halve_sum(partial_value, "row", core_bit, 1)
    col_sum = scatter_sum(core_sum, "col")
    row_piece = double_sum(col_sum, "row", [1 << 3, 3 << 3, 1 << 1, 3 << 1])
    own_share = double_join(row_piece, "row", core_bit, 1)
    pixels = img_count * lax.axis_size("row") * tile_rows * lax.axis_size("col") * tile_cols
    weight_grad = (own_share * (1.0 / math.sqrt(pixels))).T.reshape(3, 3, in_chan, share)
    features = outputs.reshape(img_count, tile_rows, tile_cols, out_chan)
    input_grad = grad_input.astype(jnp.bfloat16).reshape(img_count, tile_rows, tile_cols, in_chan)
    return (features, input_grad, weight_grad)


def solution(mesh):
    placed = (
        P("row", "col", None, None),
        P(None, None, None, "col"),
        P(),
        P("row", "col", None, None),
    )
    return jax.shard_map(
        on_device,
        mesh=mesh,
        in_specs=placed,
        out_specs=(
            P("row", "col", None, None),
            P("row", "col", None, None),
            P(None, None, None, "col"),
        ),
        check_vma=False,
    )
```

```python
import math

import jax
import jax.numpy as jnp
from jax import lax
from jax.sharding import PartitionSpec as P

epsilon = 1e-06
root_half = 0.7071067811865476
norm_const = 0.3989422804014327


def padded_2(value, sides, width):
    for axis, dim in sides:
        peers, length = (lax.axis_size(axis), value.shape[dim])
        up = [(i, (i + 1) % peers) for i in range(peers - 1)]
        down = [(j, i) for i, j in up]
        last = lax.slice_in_dim(value, length - width, length, axis=dim)
        initial = lax.slice_in_dim(value, 0, width, axis=dim)
        before = lax.ppermute(last, axis, up)
        after = lax.ppermute(initial, axis, down)
        value = jnp.concatenate([before, value, after], axis=dim)
    return value


def exchange(value, axis, bit, mask=None):
    peers = lax.axis_size(axis)
    mask = 1 << bit if mask is None else mask
    pairs = [(i, i ^ mask) for i in range(peers)]
    return lax.ppermute(value, axis, pairs)


def gather_chunks(value, axis):
    peers = lax.axis_size(axis)
    copies = jnp.broadcast_to(value[None], (peers,) + value.shape)
    return lax.all_to_all(copies, axis, 0, 0, tiled=False)


def scatter_sum(value, axis):
    peers = lax.axis_size(axis)
    blocks = value.reshape((peers, value.shape[0] // peers) + value.shape[1:])
    return lax.all_to_all(blocks, axis, 0, 0, tiled=False).sum(0)


def split_pair(value, upper, dim):
    low, high = jnp.split(value, 2, axis=dim)
    return jnp.where(upper, high, low), jnp.where(upper, low, high)


def join_pair(value, other, upper, dim):
    return jnp.where(upper, jnp.concatenate([other, value], dim), jnp.concatenate([value, other], dim))


def halve_sum(value, axis, bits, dim):
    me = lax.axis_index(axis)
    for bit in bits:
        keep, send = split_pair(value, ((me >> bit) & 1) == 1, dim)
        value = keep + exchange(send, axis, bit)
    return value


def double_sum(value, axis, masks):
    for mask in masks:
        value = value + exchange(value, axis, 0, mask)
    return value


def double_join(value, axis, bits, dim):
    me = lax.axis_index(axis)
    for bit in bits:
        value = join_pair(value, exchange(value, axis, bit), ((me >> bit) & 1) == 1, dim)
    return value


def norm_act(conv_out, upper, norm_gain):
    mean_val = jnp.mean(conv_out, axis=-1, keepdims=True)
    centred = conv_out - mean_val
    variance = jnp.mean(centred * centred, axis=-1, keepdims=True)
    inv_std = lax.rsqrt(variance + epsilon)
    unit = centred * inv_std
    normed = unit * norm_gain
    cdf_val = 0.5 * (1.0 + lax.erf(normed * root_half))
    density = jnp.exp(-0.5 * normed * normed) * norm_const
    outputs = (normed * cdf_val).astype(jnp.bfloat16)
    upstream = upper.astype(jnp.float32) * (cdf_val + normed * density) * norm_gain
    mean_up = jnp.mean(upstream, axis=-1, keepdims=True)
    mean_cross = jnp.mean(upstream * unit, axis=-1, keepdims=True)
    grad_pre = inv_std * (upstream - mean_up - unit * mean_cross)
    return (outputs, grad_pre.astype(jnp.bfloat16))


def window(padded, tap_row, tap_col, tile_rows, tile_cols):
    return padded[:, tap_row : tap_row + tile_rows, tap_col : tap_col + tile_cols, :].reshape(
        -1, padded.shape[-1]
    )


def on_device(images, weight, norm_gain, cotangent):
    img_count, tile_rows, tile_cols, in_chan = images.shape
    taps, share = 9 * in_chan, weight.shape[3]
    local_t = weight.reshape(taps, share).T
    core_bit = [0]
    half_t, _ = split_pair(local_t, (lax.axis_index("row") & 1) == 1, 1)
    kernel_t = double_join(gather_chunks(half_t, "col"), "row", core_bit, 2).reshape(-1, taps)
    out_chan = kernel_t.shape[0]
    whole_kernel = kernel_t.T.reshape(3, 3, in_chan, out_chan)
    rimmed = padded_2(images, (("col", 1),), 1)
    padded = jnp.pad(rimmed, ((0, 0), (0, 0), (1, 1), (0, 0)))
    conv_out = jnp.zeros((img_count * tile_rows * tile_cols, out_chan), jnp.float32)
    for tap_row in range(3):
        for tap_col in range(3):
            conv_out = conv_out + jnp.dot(
                window(padded, tap_row, tap_col, tile_rows, tile_cols),
                whole_kernel[tap_row, tap_col],
                preferred_element_type=jnp.float32,
            )
    outputs, grad_pre = norm_act(conv_out, cotangent.reshape(-1, out_chan), norm_gain)
    grad_grid = grad_pre.reshape(img_count, tile_rows, tile_cols, out_chan)
    grad_rimmed = padded_2(grad_grid, (("col", 1),), 1)
    grad_pad = jnp.pad(grad_rimmed, ((0, 0), (0, 0), (1, 1), (0, 0)))
    grad_input = jnp.zeros((img_count * tile_rows * tile_cols, in_chan), jnp.float32)
    pieces = []
    for tap_row in range(3):
        for tap_col in range(3):
            grad_input = grad_input + lax.dot_general(
                window(grad_pad, 2 - tap_row, 2 - tap_col, tile_rows, tile_cols),
                whole_kernel[tap_row, tap_col],
                (((1,), (1,)), ((), ())),
                preferred_element_type=jnp.float32,
            )
            pieces.append(
                lax.dot_general(
                    grad_pre,
                    window(padded, tap_row, tap_col, tile_rows, tile_cols),
                    (((0,), (0,)), ((), ())),
                    preferred_element_type=jnp.float32,
                )
            )
    partial_value = jnp.stack(pieces, axis=1).reshape(out_chan, taps)
    core_sum = halve_sum(partial_value, "row", core_bit, 1)
    ring_x = lax.axis_index("row") >> 3
    x_upper = ((ring_x ^ (ring_x >> 1)) & 1) == 1
    keep, send = split_pair(core_sum, x_upper, 1)
    x_sum = keep + exchange(send, "row", 0, 1 << 3)
    col_sum = scatter_sum(x_sum, "col")
    row_piece = double_sum(col_sum, "row", [3 << 3, 1 << 1, 3 << 1])
    x_joined = join_pair(row_piece, exchange(row_piece, "row", 0, 1 << 3), x_upper, 1)
    own_share = double_join(x_joined, "row", core_bit, 1)
    pixels = img_count * lax.axis_size("row") * tile_rows * lax.axis_size("col") * tile_cols
    weight_grad = (own_share * (1.0 / math.sqrt(pixels))).T.reshape(3, 3, in_chan, share)
    features = outputs.reshape(img_count, tile_rows, tile_cols, out_chan)
    input_grad = grad_input.astype(jnp.bfloat16).reshape(img_count, tile_rows, tile_cols, in_chan)
    return (features, input_grad, weight_grad)


def solution(mesh):
    placed = (
        P("row", "col", None, None),
        P(None, None, None, "col"),
        P(),
        P("row", "col", None, None),
    )
    return jax.shard_map(
        on_device,
        mesh=mesh,
        in_specs=placed,
        out_specs=(
            P("row", "col", None, None),
            P("row", "col", None, None),
            P(None, None, None, "col"),
        ),
        check_vma=False,
    )
```

```python
import math

import jax
import jax.numpy as jnp
from jax import lax
from jax.sharding import PartitionSpec as P

epsilon = 1e-06
root_half = 0.7071067811865476
norm_const = 0.3989422804014327


def padded_2(value, sides, width):
    for axis, dim in sides:
        peers, length = (lax.axis_size(axis), value.shape[dim])
        up = [(i, (i + 1) % peers) for i in range(peers - 1)]
        down = [(j, i) for i, j in up]
        last = lax.slice_in_dim(value, length - width, length, axis=dim)
        initial = lax.slice_in_dim(value, 0, width, axis=dim)
        before = lax.ppermute(last, axis, up)
        after = lax.ppermute(initial, axis, down)
        value = jnp.concatenate([before, value, after], axis=dim)
    return value


def exchange(value, axis, bit, mask=None):
    peers = lax.axis_size(axis)
    mask = 1 << bit if mask is None else mask
    pairs = [(i, i ^ mask) for i in range(peers)]
    return lax.ppermute(value, axis, pairs)


def gather_chunks(value, axis):
    peers = lax.axis_size(axis)
    copies = jnp.broadcast_to(value[None], (peers,) + value.shape)
    return lax.all_to_all(copies, axis, 0, 0, tiled=False)


def scatter_sum(value, axis):
    peers = lax.axis_size(axis)
    blocks = value.reshape((peers, value.shape[0] // peers) + value.shape[1:])
    return lax.all_to_all(blocks, axis, 0, 0, tiled=False).sum(0)


def split_pair(value, upper, dim):
    low, high = jnp.split(value, 2, axis=dim)
    return jnp.where(upper, high, low), jnp.where(upper, low, high)


def join_pair(value, other, upper, dim):
    return jnp.where(upper, jnp.concatenate([other, value], dim), jnp.concatenate([value, other], dim))


def halve_sum(value, axis, bits, dim):
    me = lax.axis_index(axis)
    for bit in bits:
        keep, send = split_pair(value, ((me >> bit) & 1) == 1, dim)
        value = keep + exchange(send, axis, bit)
    return value


def double_sum(value, axis, masks):
    for mask in masks:
        value = value + exchange(value, axis, 0, mask)
    return value


def double_join(value, axis, bits, dim):
    me = lax.axis_index(axis)
    for bit in bits:
        value = join_pair(value, exchange(value, axis, bit), ((me >> bit) & 1) == 1, dim)
    return value


def norm_act(conv_out, upper, norm_gain):
    mean_val = jnp.mean(conv_out, axis=-1, keepdims=True)
    centred = conv_out - mean_val
    variance = jnp.mean(centred * centred, axis=-1, keepdims=True)
    inv_std = lax.rsqrt(variance + epsilon)
    unit = centred * inv_std
    normed = unit * norm_gain
    cdf_val = 0.5 * (1.0 + lax.erf(normed * root_half))
    density = jnp.exp(-0.5 * normed * normed) * norm_const
    outputs = (normed * cdf_val).astype(jnp.bfloat16)
    upstream = upper.astype(jnp.float32) * (cdf_val + normed * density) * norm_gain
    mean_up = jnp.mean(upstream, axis=-1, keepdims=True)
    mean_cross = jnp.mean(upstream * unit, axis=-1, keepdims=True)
    grad_pre = inv_std * (upstream - mean_up - unit * mean_cross)
    return (outputs, grad_pre.astype(jnp.bfloat16))


def window(padded, tap_row, tap_col, tile_rows, tile_cols):
    return padded[:, tap_row : tap_row + tile_rows, tap_col : tap_col + tile_cols, :].reshape(
        -1, padded.shape[-1]
    )


def on_device(images, weight, norm_gain, cotangent):
    img_count, tile_rows, tile_cols, in_chan = images.shape
    taps, share = 9 * in_chan, weight.shape[3]
    local_t = weight.reshape(taps, share).T
    core_bit = [0]
    half_t, _ = split_pair(local_t, (lax.axis_index("row") & 1) == 1, 1)
    kernel_t = double_join(gather_chunks(half_t, "col"), "row", core_bit, 2).reshape(-1, taps)
    out_chan = kernel_t.shape[0]
    whole_kernel = kernel_t.T.reshape(3, 3, in_chan, out_chan)
    rimmed = padded_2(images, (("col", 1),), 1)
    padded = jnp.pad(rimmed, ((0, 0), (0, 0), (1, 1), (0, 0)))
    spec = ("NHWC", "HWIO", "NHWC")
    conv_out = lax.conv_general_dilated(
        padded, whole_kernel, (1, 1), "VALID", dimension_numbers=spec, preferred_element_type=jnp.float32
    ).reshape(-1, out_chan)
    outputs, grad_pre = norm_act(conv_out, cotangent.reshape(-1, out_chan), norm_gain)
    grad_grid = grad_pre.reshape(img_count, tile_rows, tile_cols, out_chan)
    grad_rimmed = padded_2(grad_grid, (("col", 1),), 1)
    grad_pad = jnp.pad(grad_rimmed, ((0, 0), (0, 0), (1, 1), (0, 0)))
    flipped = kernel_t.reshape(out_chan, 3, 3, in_chan)[:, ::-1, ::-1, :]
    grad_input = lax.conv_general_dilated(
        grad_pad, flipped, (1, 1), "VALID", dimension_numbers=("NHWC", "IHWO", "NHWC"),
        preferred_element_type=jnp.float32,
    ).reshape(-1, in_chan)
    partial_value = lax.conv_general_dilated(
        padded, grad_grid, (1, 1), "VALID", dimension_numbers=("CHWN", "IHWO", "CHWN"),
        preferred_element_type=jnp.float32,
    ).reshape(out_chan, taps)
    core_sum = halve_sum(partial_value, "row", core_bit, 1)
    col_sum = scatter_sum(core_sum, "col")
    row_piece = double_sum(col_sum, "row", [1 << 3, 3 << 3, 1 << 1, 3 << 1])
    own_share = double_join(row_piece, "row", core_bit, 1)
    pixels = img_count * lax.axis_size("row") * tile_rows * lax.axis_size("col") * tile_cols
    weight_grad = (own_share * (1.0 / math.sqrt(pixels))).T.reshape(3, 3, in_chan, share)
    features = outputs.reshape(img_count, tile_rows, tile_cols, out_chan)
    input_grad = grad_input.astype(jnp.bfloat16).reshape(img_count, tile_rows, tile_cols, in_chan)
    return (features, input_grad, weight_grad)


def solution(mesh):
    placed = (
        P("row", "col", None, None),
        P(None, None, None, "col"),
        P(),
        P("row", "col", None, None),
    )
    return jax.shard_map(
        on_device,
        mesh=mesh,
        in_specs=placed,
        out_specs=(
            P("row", "col", None, None),
            P("row", "col", None, None),
            P(None, None, None, "col"),
        ),
        check_vma=False,
    )
```

```python
import math

import jax
import jax.numpy as jnp
from jax import lax
from jax.sharding import PartitionSpec as P

epsilon = 1e-06
root_half = 0.7071067811865476
norm_const = 0.3989422804014327


def padded_2(value, sides, width):
    for axis, dim in sides:
        peers, length = (lax.axis_size(axis), value.shape[dim])
        up = [(i, (i + 1) % peers) for i in range(peers - 1)]
        down = [(j, i) for i, j in up]
        last = lax.slice_in_dim(value, length - width, length, axis=dim)
        initial = lax.slice_in_dim(value, 0, width, axis=dim)
        before = lax.ppermute(last, axis, up)
        after = lax.ppermute(initial, axis, down)
        value = jnp.concatenate([before, value, after], axis=dim)
    return value


def exchange(value, axis, bit, mask=None):
    peers = lax.axis_size(axis)
    mask = 1 << bit if mask is None else mask
    pairs = [(i, i ^ mask) for i in range(peers)]
    return lax.ppermute(value, axis, pairs)


def gather_chunks(value, axis):
    peers = lax.axis_size(axis)
    copies = jnp.broadcast_to(value[None], (peers,) + value.shape)
    return lax.all_to_all(copies, axis, 0, 0, tiled=False)


def scatter_sum(value, axis):
    peers = lax.axis_size(axis)
    blocks = value.reshape((peers, value.shape[0] // peers) + value.shape[1:])
    return lax.all_to_all(blocks, axis, 0, 0, tiled=False).sum(0)


def split_pair(value, upper, dim):
    low, high = jnp.split(value, 2, axis=dim)
    return jnp.where(upper, high, low), jnp.where(upper, low, high)


def join_pair(value, other, upper, dim):
    return jnp.where(upper, jnp.concatenate([other, value], dim), jnp.concatenate([value, other], dim))


def halve_sum(value, axis, bits, dim):
    me = lax.axis_index(axis)
    for bit in bits:
        keep, send = split_pair(value, ((me >> bit) & 1) == 1, dim)
        value = keep + exchange(send, axis, bit)
    return value


def double_sum(value, axis, masks):
    for mask in masks:
        value = value + exchange(value, axis, 0, mask)
    return value


def double_join(value, axis, bits, dim):
    me = lax.axis_index(axis)
    for bit in bits:
        value = join_pair(value, exchange(value, axis, bit), ((me >> bit) & 1) == 1, dim)
    return value


def norm_act(conv_out, upper, norm_gain):
    mean_val = jnp.mean(conv_out, axis=-1, keepdims=True)
    centred = conv_out - mean_val
    variance = jnp.mean(centred * centred, axis=-1, keepdims=True)
    inv_std = lax.rsqrt(variance + epsilon)
    unit = centred * inv_std
    normed = unit * norm_gain
    cdf_val = 0.5 * (1.0 + lax.erf(normed * root_half))
    density = jnp.exp(-0.5 * normed * normed) * norm_const
    outputs = (normed * cdf_val).astype(jnp.bfloat16)
    upstream = upper.astype(jnp.float32) * (cdf_val + normed * density) * norm_gain
    mean_up = jnp.mean(upstream, axis=-1, keepdims=True)
    mean_cross = jnp.mean(upstream * unit, axis=-1, keepdims=True)
    grad_pre = inv_std * (upstream - mean_up - unit * mean_cross)
    return (outputs, grad_pre.astype(jnp.bfloat16))


def window(padded, tap_row, tap_col, tile_rows, tile_cols):
    return padded[:, tap_row : tap_row + tile_rows, tap_col : tap_col + tile_cols, :].reshape(
        -1, padded.shape[-1]
    )


def on_device(images, weight, norm_gain, cotangent):
    img_count, tile_rows, tile_cols, in_chan = images.shape
    taps, share = 9 * in_chan, weight.shape[3]
    local_t = weight.reshape(taps, share).T
    core_bit = [0]
    half_t, _ = split_pair(local_t, (lax.axis_index("row") & 1) == 1, 1)
    kernel_t = double_join(gather_chunks(half_t, "col"), "row", core_bit, 2).reshape(-1, taps)
    out_chan = kernel_t.shape[0]
    whole_kernel = kernel_t.T.reshape(3, 3, in_chan, out_chan)
    rimmed = padded_2(images, (("col", 1),), 1)
    padded = jnp.pad(rimmed, ((0, 0), (0, 0), (1, 1), (0, 0)))
    spec = ("NHWC", "HWIO", "NHWC")
    conv_out = lax.conv_general_dilated(
        padded, whole_kernel, (1, 1), "VALID", dimension_numbers=spec, preferred_element_type=jnp.float32
    ).reshape(-1, out_chan)
    outputs, grad_pre = norm_act(conv_out, cotangent.reshape(-1, out_chan), norm_gain)
    grad_grid = grad_pre.reshape(img_count, tile_rows, tile_cols, out_chan)
    grad_rimmed = padded_2(grad_grid, (("col", 1),), 1)
    grad_pad = jnp.pad(grad_rimmed, ((0, 0), (0, 0), (1, 1), (0, 0)))
    flipped = kernel_t.reshape(out_chan, 3, 3, in_chan)[:, ::-1, ::-1, :]
    grad_input = lax.conv_general_dilated(
        grad_pad, flipped, (1, 1), "VALID", dimension_numbers=("NHWC", "IHWO", "NHWC"),
        preferred_element_type=jnp.float32,
    ).reshape(-1, in_chan)
    pieces = [
        lax.dot_general(
            grad_pre,
            window(padded, tap_row, tap_col, tile_rows, tile_cols),
            (((0,), (0,)), ((), ())),
            preferred_element_type=jnp.float32,
        )
        for tap_row in range(3)
        for tap_col in range(3)
    ]
    partial_value = jnp.stack(pieces, axis=1).reshape(out_chan, taps)
    core_sum = halve_sum(partial_value, "row", core_bit, 1)
    col_sum = scatter_sum(core_sum, "col")
    row_piece = double_sum(col_sum, "row", [1 << 3, 3 << 3, 1 << 1, 3 << 1])
    own_share = double_join(row_piece, "row", core_bit, 1)
    pixels = img_count * lax.axis_size("row") * tile_rows * lax.axis_size("col") * tile_cols
    weight_grad = (own_share * (1.0 / math.sqrt(pixels))).T.reshape(3, 3, in_chan, share)
    features = outputs.reshape(img_count, tile_rows, tile_cols, out_chan)
    input_grad = grad_input.astype(jnp.bfloat16).reshape(img_count, tile_rows, tile_cols, in_chan)
    return (features, input_grad, weight_grad)


def solution(mesh):
    placed = (
        P("row", "col", None, None),
        P(None, None, None, "col"),
        P(),
        P("row", "col", None, None),
    )
    return jax.shard_map(
        on_device,
        mesh=mesh,
        in_specs=placed,
        out_specs=(
            P("row", "col", None, None),
            P("row", "col", None, None),
            P(None, None, None, "col"),
        ),
        check_vma=False,
    )
```

```python
import math

import jax
import jax.numpy as jnp
from jax import lax
from jax.sharding import PartitionSpec as P

epsilon = 1e-06
root_half = 0.7071067811865476
norm_const = 0.3989422804014327


def padded_2(value, sides, width):
    for axis, dim in sides:
        peers, length = (lax.axis_size(axis), value.shape[dim])
        up = [(i, (i + 1) % peers) for i in range(peers - 1)]
        down = [(j, i) for i, j in up]
        last = lax.slice_in_dim(value, length - width, length, axis=dim)
        initial = lax.slice_in_dim(value, 0, width, axis=dim)
        before = lax.ppermute(last, axis, up)
        after = lax.ppermute(initial, axis, down)
        value = jnp.concatenate([before, value, after], axis=dim)
    return value


def exchange(value, axis, bit, mask=None):
    peers = lax.axis_size(axis)
    mask = 1 << bit if mask is None else mask
    pairs = [(i, i ^ mask) for i in range(peers)]
    return lax.ppermute(value, axis, pairs)


def gather_chunks(value, axis):
    peers = lax.axis_size(axis)
    copies = jnp.broadcast_to(value[None], (peers,) + value.shape)
    return lax.all_to_all(copies, axis, 0, 0, tiled=False)


def scatter_sum(value, axis):
    peers = lax.axis_size(axis)
    blocks = value.reshape((peers, value.shape[0] // peers) + value.shape[1:])
    return lax.all_to_all(blocks, axis, 0, 0, tiled=False).sum(0)


def split_pair(value, upper, dim):
    low, high = jnp.split(value, 2, axis=dim)
    return jnp.where(upper, high, low), jnp.where(upper, low, high)


def join_pair(value, other, upper, dim):
    return jnp.where(upper, jnp.concatenate([other, value], dim), jnp.concatenate([value, other], dim))


def halve_sum(value, axis, bits, dim):
    me = lax.axis_index(axis)
    for bit in bits:
        keep, send = split_pair(value, ((me >> bit) & 1) == 1, dim)
        value = keep + exchange(send, axis, bit)
    return value


def double_sum(value, axis, masks):
    for mask in masks:
        value = value + exchange(value, axis, 0, mask)
    return value


def double_join(value, axis, bits, dim):
    me = lax.axis_index(axis)
    for bit in bits:
        value = join_pair(value, exchange(value, axis, bit), ((me >> bit) & 1) == 1, dim)
    return value


def norm_act(conv_out, upper, norm_gain):
    mean_val = jnp.mean(conv_out, axis=-1, keepdims=True)
    centred = conv_out - mean_val
    variance = jnp.mean(centred * centred, axis=-1, keepdims=True)
    inv_std = lax.rsqrt(variance + epsilon)
    unit = centred * inv_std
    normed = unit * norm_gain
    cdf_val = 0.5 * (1.0 + lax.erf(normed * root_half))
    density = jnp.exp(-0.5 * normed * normed) * norm_const
    outputs = (normed * cdf_val).astype(jnp.bfloat16)
    upstream = upper.astype(jnp.float32) * (cdf_val + normed * density) * norm_gain
    mean_up = jnp.mean(upstream, axis=-1, keepdims=True)
    mean_cross = jnp.mean(upstream * unit, axis=-1, keepdims=True)
    grad_pre = inv_std * (upstream - mean_up - unit * mean_cross)
    return (outputs, grad_pre.astype(jnp.bfloat16))


def window(padded, tap_row, tap_col, tile_rows, tile_cols):
    return padded[:, tap_row : tap_row + tile_rows, tap_col : tap_col + tile_cols, :].reshape(
        -1, padded.shape[-1]
    )


def on_device(images, weight, norm_gain, cotangent):
    img_count, tile_rows, tile_cols, in_chan = images.shape
    taps, share = 9 * in_chan, weight.shape[3]
    local_t = weight.reshape(taps, share).T
    core_bit = [0]
    half_t, _ = split_pair(local_t, (lax.axis_index("row") & 1) == 1, 1)
    rimmed = padded_2(images, (("col", 1),), 1)
    rimmed, half_t = lax.optimization_barrier((rimmed, half_t))
    kernel_t = double_join(gather_chunks(half_t, "col"), "row", core_bit, 2).reshape(-1, taps)
    out_chan = kernel_t.shape[0]
    whole_kernel = kernel_t.T.reshape(3, 3, in_chan, out_chan)
    padded = jnp.pad(rimmed, ((0, 0), (0, 0), (1, 1), (0, 0)))
    conv_out = lax.conv_general_dilated(
        padded, whole_kernel, (1, 1), "VALID", dimension_numbers=("NHWC", "HWIO", "NHWC"),
        preferred_element_type=jnp.float32,
    ).reshape(-1, out_chan)
    outputs, grad_pre = norm_act(conv_out, cotangent.reshape(-1, out_chan), norm_gain)
    grad_grid = grad_pre.reshape(img_count, tile_rows, tile_cols, out_chan)
    grad_rimmed = padded_2(grad_grid, (("col", 1),), 1)
    grad_pad = jnp.pad(grad_rimmed, ((0, 0), (0, 0), (1, 1), (0, 0)))
    grad_input = jnp.zeros((img_count * tile_rows * tile_cols, in_chan), jnp.float32)
    pieces = []
    for tap_row in range(3):
        for tap_col in range(3):
            grad_input = grad_input + lax.dot_general(
                window(grad_pad, 2 - tap_row, 2 - tap_col, tile_rows, tile_cols),
                whole_kernel[tap_row, tap_col],
                (((1,), (1,)), ((), ())),
                preferred_element_type=jnp.float32,
            )
            pieces.append(
                lax.dot_general(
                    grad_pre,
                    window(padded, tap_row, tap_col, tile_rows, tile_cols),
                    (((0,), (0,)), ((), ())),
                    preferred_element_type=jnp.float32,
                )
            )
    partial_value = jnp.stack(pieces, axis=1).reshape(out_chan, taps)
    core_sum = halve_sum(partial_value, "row", core_bit, 1)
    col_sum = scatter_sum(core_sum, "col")
    row_piece = double_sum(col_sum, "row", [1 << 3, 3 << 3, 1 << 1, 3 << 1])
    own_share = double_join(row_piece, "row", core_bit, 1)
    pixels = img_count * lax.axis_size("row") * tile_rows * lax.axis_size("col") * tile_cols
    weight_grad = (own_share * (1.0 / math.sqrt(pixels))).T.reshape(3, 3, in_chan, share)
    features = outputs.reshape(img_count, tile_rows, tile_cols, out_chan)
    input_grad = grad_input.astype(jnp.bfloat16).reshape(img_count, tile_rows, tile_cols, in_chan)
    return (features, input_grad, weight_grad)


def solution(mesh):
    placed = (
        P("row", "col", None, None),
        P(None, None, None, "col"),
        P(),
        P("row", "col", None, None),
    )
    return jax.shard_map(
        on_device,
        mesh=mesh,
        in_specs=placed,
        out_specs=(
            P("row", "col", None, None),
            P("row", "col", None, None),
            P(None, None, None, "col"),
        ),
        check_vma=False,
    )
```

```python
import math

import jax
import jax.numpy as jnp
from jax import lax
from jax.sharding import PartitionSpec as P

epsilon = 1e-06
root_half = 0.7071067811865476
norm_const = 0.3989422804014327


def padded_2(value, sides, width):
    for axis, dim in sides:
        peers, length = (lax.axis_size(axis), value.shape[dim])
        up = [(i, (i + 1) % peers) for i in range(peers - 1)]
        down = [(j, i) for i, j in up]
        last = lax.slice_in_dim(value, length - width, length, axis=dim)
        initial = lax.slice_in_dim(value, 0, width, axis=dim)
        before = lax.ppermute(last, axis, up)
        after = lax.ppermute(initial, axis, down)
        value = jnp.concatenate([before, value, after], axis=dim)
    return value


def exchange(value, axis, bit, mask=None):
    peers = lax.axis_size(axis)
    mask = 1 << bit if mask is None else mask
    pairs = [(i, i ^ mask) for i in range(peers)]
    return lax.ppermute(value, axis, pairs)


def gather_chunks(value, axis):
    peers = lax.axis_size(axis)
    copies = jnp.broadcast_to(value[None], (peers,) + value.shape)
    return lax.all_to_all(copies, axis, 0, 0, tiled=False)


def scatter_sum(value, axis):
    peers = lax.axis_size(axis)
    blocks = value.reshape((peers, value.shape[0] // peers) + value.shape[1:])
    return lax.all_to_all(blocks, axis, 0, 0, tiled=False).sum(0)


def split_pair(value, upper, dim):
    low, high = jnp.split(value, 2, axis=dim)
    return jnp.where(upper, high, low), jnp.where(upper, low, high)


def join_pair(value, other, upper, dim):
    return jnp.where(upper, jnp.concatenate([other, value], dim), jnp.concatenate([value, other], dim))


def halve_sum(value, axis, bits, dim):
    me = lax.axis_index(axis)
    for bit in bits:
        keep, send = split_pair(value, ((me >> bit) & 1) == 1, dim)
        value = keep + exchange(send, axis, bit)
    return value


def double_sum(value, axis, masks):
    for mask in masks:
        value = value + exchange(value, axis, 0, mask)
    return value


def double_join(value, axis, bits, dim):
    me = lax.axis_index(axis)
    for bit in bits:
        value = join_pair(value, exchange(value, axis, bit), ((me >> bit) & 1) == 1, dim)
    return value


def norm_act(conv_out, upper, norm_gain):
    mean_val = jnp.mean(conv_out, axis=-1, keepdims=True)
    centred = conv_out - mean_val
    variance = jnp.mean(centred * centred, axis=-1, keepdims=True)
    inv_std = lax.rsqrt(variance + epsilon)
    unit = centred * inv_std
    normed = unit * norm_gain
    cdf_val = 0.5 * (1.0 + lax.erf(normed * root_half))
    density = jnp.exp(-0.5 * normed * normed) * norm_const
    outputs = (normed * cdf_val).astype(jnp.bfloat16)
    upstream = upper.astype(jnp.float32) * (cdf_val + normed * density) * norm_gain
    mean_up = jnp.mean(upstream, axis=-1, keepdims=True)
    mean_cross = jnp.mean(upstream * unit, axis=-1, keepdims=True)
    grad_pre = inv_std * (upstream - mean_up - unit * mean_cross)
    return (outputs, grad_pre.astype(jnp.bfloat16))


def window(padded, tap_row, tap_col, tile_rows, tile_cols):
    return padded[:, tap_row : tap_row + tile_rows, tap_col : tap_col + tile_cols, :].reshape(
        -1, padded.shape[-1]
    )


def on_device(images, weight, norm_gain, cotangent):
    img_count, tile_rows, tile_cols, in_chan = images.shape
    taps, share = 9 * in_chan, weight.shape[3]
    local_t = weight.reshape(taps, share).T
    core_bit = [0]
    half_t, _ = split_pair(local_t, (lax.axis_index("row") & 1) == 1, 1)
    kernel_t = double_join(gather_chunks(half_t, "col"), "row", core_bit, 2).reshape(-1, taps)
    out_chan = kernel_t.shape[0]
    whole_kernel = kernel_t.T.reshape(3, 3, in_chan, out_chan)
    rimmed = padded_2(images, (("col", 1),), 1)
    padded = jnp.pad(rimmed, ((0, 0), (0, 0), (1, 1), (0, 0)))
    conv_out = jnp.zeros((img_count * tile_rows * tile_cols, out_chan), jnp.float32)
    for tap_row in range(3):
        for tap_col in range(3):
            conv_out = conv_out + jnp.dot(
                window(padded, tap_row, tap_col, tile_rows, tile_cols),
                whole_kernel[tap_row, tap_col],
                preferred_element_type=jnp.float32,
            )
    outputs, grad_pre = norm_act(conv_out, cotangent.reshape(-1, out_chan), norm_gain)
    grad_grid = grad_pre.reshape(img_count, tile_rows, tile_cols, out_chan)
    grad_rimmed = padded_2(grad_grid, (("col", 1),), 1)
    grad_pad = jnp.pad(grad_rimmed, ((0, 0), (0, 0), (1, 1), (0, 0)))
    grad_input = jnp.zeros((img_count * tile_rows * tile_cols, in_chan), jnp.float32)
    pieces = []
    for tap_row in range(3):
        for tap_col in range(3):
            grad_input = grad_input + lax.dot_general(
                window(grad_pad, 2 - tap_row, 2 - tap_col, tile_rows, tile_cols),
                whole_kernel[tap_row, tap_col],
                (((1,), (1,)), ((), ())),
                preferred_element_type=jnp.float32,
            )
            pieces.append(
                lax.dot_general(
                    grad_pre,
                    window(padded, tap_row, tap_col, tile_rows, tile_cols),
                    (((0,), (0,)), ((), ())),
                    preferred_element_type=jnp.float32,
                )
            )
    partial_value = jnp.stack(pieces, axis=1).reshape(out_chan, taps)
    core_sum = halve_sum(partial_value, "row", core_bit, 1)
    col_sum = scatter_sum(core_sum, "col")
    row_piece = double_sum(col_sum, "row", [1 << 1, 3 << 1, 1 << 3, 3 << 3])
    own_share = double_join(row_piece, "row", core_bit, 1)
    pixels = img_count * lax.axis_size("row") * tile_rows * lax.axis_size("col") * tile_cols
    weight_grad = (own_share * (1.0 / math.sqrt(pixels))).T.reshape(3, 3, in_chan, share)
    features = outputs.reshape(img_count, tile_rows, tile_cols, out_chan)
    input_grad = grad_input.astype(jnp.bfloat16).reshape(img_count, tile_rows, tile_cols, in_chan)
    return (features, input_grad, weight_grad)


def solution(mesh):
    placed = (
        P("row", "col", None, None),
        P(None, None, None, "col"),
        P(),
        P("row", "col", None, None),
    )
    return jax.shard_map(
        on_device,
        mesh=mesh,
        in_specs=placed,
        out_specs=(
            P("row", "col", None, None),
            P("row", "col", None, None),
            P(None, None, None, "col"),
        ),
        check_vma=False,
    )
```

```python
import math

import jax
import jax.numpy as jnp
from jax import lax
from jax.sharding import PartitionSpec as P

epsilon = 1e-06
root_half = 0.7071067811865476
norm_const = 0.3989422804014327


def padded_2(value, sides, width):
    for axis, dim in sides:
        peers, length = (lax.axis_size(axis), value.shape[dim])
        up = [(i, (i + 1) % peers) for i in range(peers - 1)]
        down = [(j, i) for i, j in up]
        last = lax.slice_in_dim(value, length - width, length, axis=dim)
        initial = lax.slice_in_dim(value, 0, width, axis=dim)
        before = lax.ppermute(last, axis, up)
        after = lax.ppermute(initial, axis, down)
        value = jnp.concatenate([before, value, after], axis=dim)
    return value


def exchange(value, axis, bit, mask=None):
    peers = lax.axis_size(axis)
    mask = 1 << bit if mask is None else mask
    pairs = [(i, i ^ mask) for i in range(peers)]
    return lax.ppermute(value, axis, pairs)


def gather_chunks(value, axis):
    peers = lax.axis_size(axis)
    copies = jnp.broadcast_to(value[None], (peers,) + value.shape)
    return lax.all_to_all(copies, axis, 0, 0, tiled=False)


def scatter_sum(value, axis):
    peers = lax.axis_size(axis)
    blocks = value.reshape((peers, value.shape[0] // peers) + value.shape[1:])
    return lax.all_to_all(blocks, axis, 0, 0, tiled=False).sum(0)


def split_pair(value, upper, dim):
    low, high = jnp.split(value, 2, axis=dim)
    return jnp.where(upper, high, low), jnp.where(upper, low, high)


def join_pair(value, other, upper, dim):
    return jnp.where(upper, jnp.concatenate([other, value], dim), jnp.concatenate([value, other], dim))


def halve_sum(value, axis, bits, dim):
    me = lax.axis_index(axis)
    for bit in bits:
        keep, send = split_pair(value, ((me >> bit) & 1) == 1, dim)
        value = keep + exchange(send, axis, bit)
    return value


def double_sum(value, axis, masks):
    for mask in masks:
        value = value + exchange(value, axis, 0, mask)
    return value


def double_join(value, axis, bits, dim):
    me = lax.axis_index(axis)
    for bit in bits:
        value = join_pair(value, exchange(value, axis, bit), ((me >> bit) & 1) == 1, dim)
    return value


def norm_act(conv_out, upper, norm_gain):
    mean_val = jnp.mean(conv_out, axis=-1, keepdims=True)
    centred = conv_out - mean_val
    variance = jnp.mean(centred * centred, axis=-1, keepdims=True)
    inv_std = lax.rsqrt(variance + epsilon)
    unit = centred * inv_std
    normed = unit * norm_gain
    cdf_val = 0.5 * (1.0 + lax.erf(normed * root_half))
    density = jnp.exp(-0.5 * normed * normed) * norm_const
    outputs = (normed * cdf_val).astype(jnp.bfloat16)
    upstream = upper.astype(jnp.float32) * (cdf_val + normed * density) * norm_gain
    mean_up = jnp.mean(upstream, axis=-1, keepdims=True)
    mean_cross = jnp.mean(upstream * unit, axis=-1, keepdims=True)
    grad_pre = inv_std * (upstream - mean_up - unit * mean_cross)
    return (outputs, grad_pre.astype(jnp.bfloat16))


def window(padded, tap_row, tap_col, tile_rows, tile_cols):
    return padded[:, tap_row : tap_row + tile_rows, tap_col : tap_col + tile_cols, :].reshape(
        -1, padded.shape[-1]
    )


def on_device(images, weight, norm_gain, cotangent):
    img_count, tile_rows, tile_cols, in_chan = images.shape
    taps, share = 9 * in_chan, weight.shape[3]
    local_t = weight.reshape(taps, share).T
    core_bit = [0]
    half_t, _ = split_pair(local_t, (lax.axis_index("row") & 1) == 1, 1)
    kernel_t = double_join(gather_chunks(half_t, "col"), "row", core_bit, 2).reshape(-1, taps)
    out_chan = kernel_t.shape[0]
    whole_kernel = kernel_t.T.reshape(3, 3, in_chan, out_chan)
    rimmed = padded_2(images, (("col", 1),), 1)
    padded = jnp.pad(rimmed, ((0, 0), (0, 0), (1, 1), (0, 0)))
    conv_out = jnp.zeros((img_count * tile_rows * tile_cols, out_chan), jnp.float32)
    for tap_row in range(3):
        for tap_col in range(3):
            conv_out = conv_out + jnp.dot(
                window(padded, tap_row, tap_col, tile_rows, tile_cols),
                whole_kernel[tap_row, tap_col],
                preferred_element_type=jnp.float32,
            )
    outputs, grad_pre = norm_act(conv_out, cotangent.reshape(-1, out_chan), norm_gain)
    grad_grid = grad_pre.reshape(img_count, tile_rows, tile_cols, out_chan)
    grad_rimmed = padded_2(grad_grid, (("col", 1),), 1)
    grad_pad = jnp.pad(grad_rimmed, ((0, 0), (0, 0), (1, 1), (0, 0)))
    grad_input = jnp.zeros((img_count * tile_rows * tile_cols, in_chan), jnp.float32)
    pieces = []
    for tap_row in range(3):
        for tap_col in range(3):
            grad_input = grad_input + lax.dot_general(
                window(grad_pad, 2 - tap_row, 2 - tap_col, tile_rows, tile_cols),
                whole_kernel[tap_row, tap_col],
                (((1,), (1,)), ((), ())),
                preferred_element_type=jnp.float32,
            )
            pieces.append(
                lax.dot_general(
                    grad_pre,
                    window(padded, tap_row, tap_col, tile_rows, tile_cols),
                    (((0,), (0,)), ((), ())),
                    preferred_element_type=jnp.float32,
                )
            )
    partial_value = jnp.stack(pieces, axis=1).reshape(out_chan, taps)
    grad_pad, partial_value = lax.optimization_barrier((grad_pad, partial_value))
    core_sum = halve_sum(partial_value, "row", core_bit, 1)
    col_sum = scatter_sum(core_sum, "col")
    row_piece = double_sum(col_sum, "row", [1 << 1, 3 << 1, 1 << 3, 3 << 3])
    own_share = double_join(row_piece, "row", core_bit, 1)
    pixels = img_count * lax.axis_size("row") * tile_rows * lax.axis_size("col") * tile_cols
    weight_grad = (own_share * (1.0 / math.sqrt(pixels))).T.reshape(3, 3, in_chan, share)
    features = outputs.reshape(img_count, tile_rows, tile_cols, out_chan)
    input_grad = grad_input.astype(jnp.bfloat16).reshape(img_count, tile_rows, tile_cols, in_chan)
    return (features, input_grad, weight_grad)


def solution(mesh):
    placed = (
        P("row", "col", None, None),
        P(None, None, None, "col"),
        P(),
        P("row", "col", None, None),
    )
    return jax.shard_map(
        on_device,
        mesh=mesh,
        in_specs=placed,
        out_specs=(
            P("row", "col", None, None),
            P("row", "col", None, None),
            P(None, None, None, "col"),
        ),
        check_vma=False,
    )
```

```python
import math

import jax
import jax.numpy as jnp
from jax import lax
from jax.sharding import PartitionSpec as P

epsilon = 1e-06
root_half = 0.7071067811865476
norm_const = 0.3989422804014327


def padded_2(value, sides, width):
    for axis, dim in sides:
        peers, length = (lax.axis_size(axis), value.shape[dim])
        up = [(i, (i + 1) % peers) for i in range(peers - 1)]
        down = [(j, i) for i, j in up]
        last = lax.slice_in_dim(value, length - width, length, axis=dim)
        initial = lax.slice_in_dim(value, 0, width, axis=dim)
        before = lax.ppermute(last, axis, up)
        after = lax.ppermute(initial, axis, down)
        value = jnp.concatenate([before, value, after], axis=dim)
    return value


def exchange(value, axis, bit, mask=None):
    peers = lax.axis_size(axis)
    mask = 1 << bit if mask is None else mask
    pairs = [(i, i ^ mask) for i in range(peers)]
    return lax.ppermute(value, axis, pairs)


def gather_chunks(value, axis):
    peers = lax.axis_size(axis)
    copies = jnp.broadcast_to(value[None], (peers,) + value.shape)
    return lax.all_to_all(copies, axis, 0, 0, tiled=False)


def scatter_sum(value, axis):
    peers = lax.axis_size(axis)
    blocks = value.reshape((peers, value.shape[0] // peers) + value.shape[1:])
    return lax.all_to_all(blocks, axis, 0, 0, tiled=False).sum(0)


def split_pair(value, upper, dim):
    low, high = jnp.split(value, 2, axis=dim)
    return jnp.where(upper, high, low), jnp.where(upper, low, high)


def join_pair(value, other, upper, dim):
    return jnp.where(upper, jnp.concatenate([other, value], dim), jnp.concatenate([value, other], dim))


def halve_sum(value, axis, bits, dim):
    me = lax.axis_index(axis)
    for bit in bits:
        keep, send = split_pair(value, ((me >> bit) & 1) == 1, dim)
        value = keep + exchange(send, axis, bit)
    return value


def double_sum(value, axis, masks):
    for mask in masks:
        value = value + exchange(value, axis, 0, mask)
    return value


def double_join(value, axis, bits, dim):
    me = lax.axis_index(axis)
    for bit in bits:
        value = join_pair(value, exchange(value, axis, bit), ((me >> bit) & 1) == 1, dim)
    return value


def norm_act(conv_out, upper, norm_gain):
    mean_val = jnp.mean(conv_out, axis=-1, keepdims=True)
    centred = conv_out - mean_val
    variance = jnp.mean(centred * centred, axis=-1, keepdims=True)
    inv_std = lax.rsqrt(variance + epsilon)
    unit = centred * inv_std
    normed = unit * norm_gain
    cdf_val = 0.5 * (1.0 + lax.erf(normed * root_half))
    density = jnp.exp(-0.5 * normed * normed) * norm_const
    outputs = (normed * cdf_val).astype(jnp.bfloat16)
    upstream = upper.astype(jnp.float32) * (cdf_val + normed * density) * norm_gain
    mean_up = jnp.mean(upstream, axis=-1, keepdims=True)
    mean_cross = jnp.mean(upstream * unit, axis=-1, keepdims=True)
    grad_pre = inv_std * (upstream - mean_up - unit * mean_cross)
    return (outputs, grad_pre.astype(jnp.bfloat16))


def window(padded, tap_row, tap_col, tile_rows, tile_cols):
    return padded[:, tap_row : tap_row + tile_rows, tap_col : tap_col + tile_cols, :].reshape(
        -1, padded.shape[-1]
    )


def on_device(images, weight, norm_gain, cotangent):
    img_count, tile_rows, tile_cols, in_chan = images.shape
    taps, share = 9 * in_chan, weight.shape[3]
    local_t = weight.reshape(taps, share).T
    lower = (lax.axis_index("row") & 1) == 0
    own_t = gather_chunks(jnp.where(lower, local_t[: share // 2], local_t[share // 2 :]), "col")
    mate_t = exchange(own_t, "row", 0)
    kernel_t = jnp.where(lower, jnp.concatenate([own_t, mate_t], 1), jnp.concatenate([mate_t, own_t], 1))
    kernel_t = kernel_t.reshape(-1, taps)
    out_chan = kernel_t.shape[0]
    whole_kernel = kernel_t.T.reshape(3, 3, in_chan, out_chan)
    rimmed = padded_2(images, (("col", 1),), 1)
    padded = jnp.pad(rimmed, ((0, 0), (0, 0), (1, 1), (0, 0)))
    def conv_part(part_t):
        part = part_t.reshape(-1, taps).T.reshape(3, 3, in_chan, -1)
        total = jnp.zeros((img_count * tile_rows * tile_cols, part.shape[3]), jnp.float32)
        for tap_row in range(3):
            for tap_col in range(3):
                total = total + jnp.dot(
                    window(padded, tap_row, tap_col, tile_rows, tile_cols),
                    part[tap_row, tap_col],
                    preferred_element_type=jnp.float32,
                )
        return total.reshape(total.shape[0], own_t.shape[0], 1, own_t.shape[1])

    conv_own, conv_mate = conv_part(own_t), conv_part(mate_t)
    conv_out = jnp.where(lower, jnp.concatenate([conv_own, conv_mate], 2), jnp.concatenate([conv_mate, conv_own], 2))
    conv_out = conv_out.reshape(-1, out_chan)
    outputs, grad_pre = norm_act(conv_out, cotangent.reshape(-1, out_chan), norm_gain)
    grad_grid = grad_pre.reshape(img_count, tile_rows, tile_cols, out_chan)
    grad_rimmed = padded_2(grad_grid, (("col", 1),), 1)
    grad_pad = jnp.pad(grad_rimmed, ((0, 0), (0, 0), (1, 1), (0, 0)))
    grad_input = jnp.zeros((img_count * tile_rows * tile_cols, in_chan), jnp.float32)
    pieces = []
    for tap_row in range(3):
        for tap_col in range(3):
            grad_input = grad_input + lax.dot_general(
                window(grad_pad, 2 - tap_row, 2 - tap_col, tile_rows, tile_cols),
                whole_kernel[tap_row, tap_col],
                (((1,), (1,)), ((), ())),
                preferred_element_type=jnp.float32,
            )
            pieces.append(
                lax.dot_general(
                    grad_pre,
                    window(padded, tap_row, tap_col, tile_rows, tile_cols),
                    (((0,), (0,)), ((), ())),
                    preferred_element_type=jnp.float32,
                )
            )
    partial_value = jnp.stack(pieces, axis=1).reshape(out_chan, taps)
    core_sum = halve_sum(partial_value, "row", [0], 1)
    col_sum = scatter_sum(core_sum, "col")
    row_piece = double_sum(col_sum, "row", [1 << 1, 3 << 1, 1 << 3, 3 << 3])
    own_share = double_join(row_piece, "row", [0], 1)
    pixels = img_count * lax.axis_size("row") * tile_rows * lax.axis_size("col") * tile_cols
    weight_grad = (own_share * (1.0 / math.sqrt(pixels))).T.reshape(3, 3, in_chan, share)
    features = outputs.reshape(img_count, tile_rows, tile_cols, out_chan)
    input_grad = grad_input.astype(jnp.bfloat16).reshape(img_count, tile_rows, tile_cols, in_chan)
    return (features, input_grad, weight_grad)


def solution(mesh):
    placed = (
        P("row", "col", None, None),
        P(None, None, None, "col"),
        P(),
        P("row", "col", None, None),
    )
    return jax.shard_map(
        on_device,
        mesh=mesh,
        in_specs=placed,
        out_specs=(
            P("row", "col", None, None),
            P("row", "col", None, None),
            P(None, None, None, "col"),
        ),
        check_vma=False,
    )
```

```python
import math

import jax
import jax.numpy as jnp
from jax import lax
from jax.sharding import PartitionSpec as P

epsilon = 1e-06
root_half = 0.7071067811865476
norm_const = 0.3989422804014327


def padded_2(value, sides, width):
    for axis, dim in sides:
        peers, length = (lax.axis_size(axis), value.shape[dim])
        up = [(i, (i + 1) % peers) for i in range(peers - 1)]
        down = [(j, i) for i, j in up]
        last = lax.slice_in_dim(value, length - width, length, axis=dim)
        initial = lax.slice_in_dim(value, 0, width, axis=dim)
        before = lax.ppermute(last, axis, up)
        after = lax.ppermute(initial, axis, down)
        value = jnp.concatenate([before, value, after], axis=dim)
    return value


def exchange(value, axis, bit, mask=None):
    peers = lax.axis_size(axis)
    mask = 1 << bit if mask is None else mask
    pairs = [(i, i ^ mask) for i in range(peers)]
    return lax.ppermute(value, axis, pairs)


def gather_chunks(value, axis):
    peers = lax.axis_size(axis)
    copies = jnp.broadcast_to(value[None], (peers,) + value.shape)
    return lax.all_to_all(copies, axis, 0, 0, tiled=False)


def scatter_sum(value, axis):
    peers = lax.axis_size(axis)
    blocks = value.reshape((peers, value.shape[0] // peers) + value.shape[1:])
    return lax.all_to_all(blocks, axis, 0, 0, tiled=False).sum(0)


def split_pair(value, upper, dim):
    low, high = jnp.split(value, 2, axis=dim)
    return jnp.where(upper, high, low), jnp.where(upper, low, high)


def join_pair(value, other, upper, dim):
    return jnp.where(upper, jnp.concatenate([other, value], dim), jnp.concatenate([value, other], dim))


def halve_sum(value, axis, bits, dim):
    me = lax.axis_index(axis)
    for bit in bits:
        keep, send = split_pair(value, ((me >> bit) & 1) == 1, dim)
        value = keep + exchange(send, axis, bit)
    return value


def double_sum(value, axis, masks):
    for mask in masks:
        value = value + exchange(value, axis, 0, mask)
    return value


def double_join(value, axis, bits, dim):
    me = lax.axis_index(axis)
    for bit in bits:
        value = join_pair(value, exchange(value, axis, bit), ((me >> bit) & 1) == 1, dim)
    return value


def norm_act(conv_out, upper, norm_gain):
    mean_val = jnp.mean(conv_out, axis=-1, keepdims=True)
    centred = conv_out - mean_val
    variance = jnp.mean(centred * centred, axis=-1, keepdims=True)
    inv_std = lax.rsqrt(variance + epsilon)
    unit = centred * inv_std
    normed = unit * norm_gain
    cdf_val = 0.5 * (1.0 + lax.erf(normed * root_half))
    density = jnp.exp(-0.5 * normed * normed) * norm_const
    outputs = (normed * cdf_val).astype(jnp.bfloat16)
    upstream = upper.astype(jnp.float32) * (cdf_val + normed * density) * norm_gain
    mean_up = jnp.mean(upstream, axis=-1, keepdims=True)
    mean_cross = jnp.mean(upstream * unit, axis=-1, keepdims=True)
    grad_pre = inv_std * (upstream - mean_up - unit * mean_cross)
    return (outputs, grad_pre.astype(jnp.bfloat16))


def window(padded, tap_row, tap_col, tile_rows, tile_cols):
    return padded[:, tap_row : tap_row + tile_rows, tap_col : tap_col + tile_cols, :].reshape(
        -1, padded.shape[-1]
    )


def on_device(images, weight, norm_gain, cotangent):
    img_count, tile_rows, tile_cols, in_chan = images.shape
    taps, share = 9 * in_chan, weight.shape[3]
    local_t = weight.reshape(taps, share).T
    core_bit = [0]
    half_t, _ = split_pair(local_t, (lax.axis_index("row") & 1) == 1, 1)
    kernel_t = double_join(gather_chunks(half_t, "col"), "row", core_bit, 2).reshape(-1, taps)
    out_chan = kernel_t.shape[0]
    whole_kernel = kernel_t.T.reshape(3, 3, in_chan, out_chan)
    rimmed = padded_2(images, (("col", 1),), 1)
    padded = jnp.pad(rimmed, ((0, 0), (0, 0), (1, 1), (0, 0)))
    conv_out = jnp.zeros((img_count * tile_rows * tile_cols, out_chan), jnp.float32)
    for tap_row in range(3):
        for tap_col in range(3):
            conv_out = conv_out + jnp.dot(
                window(padded, tap_row, tap_col, tile_rows, tile_cols),
                whole_kernel[tap_row, tap_col],
                preferred_element_type=jnp.float32,
            )
    outputs, grad_pre = norm_act(conv_out, cotangent.reshape(-1, out_chan), norm_gain)
    grad_grid = grad_pre.reshape(img_count, tile_rows, tile_cols, out_chan)
    grad_rimmed = padded_2(grad_grid, (("col", 1),), 1)
    grad_pad = jnp.pad(grad_rimmed, ((0, 0), (0, 0), (1, 1), (0, 0)))
    grad_input = jnp.zeros((img_count * tile_rows * tile_cols, in_chan), jnp.float32)
    pieces = []
    for tap_row in range(3):
        for tap_col in range(3):
            grad_input = grad_input + lax.dot_general(
                window(grad_pad, 2 - tap_row, 2 - tap_col, tile_rows, tile_cols),
                whole_kernel[tap_row, tap_col],
                (((1,), (1,)), ((), ())),
                preferred_element_type=jnp.float32,
            )
            pieces.append(
                lax.dot_general(
                    grad_pre,
                    window(padded, tap_row, tap_col, tile_rows, tile_cols),
                    (((0,), (0,)), ((), ())),
                    preferred_element_type=jnp.float32,
                )
            )
    pixels = img_count * lax.axis_size("row") * tile_rows * lax.axis_size("col") * tile_cols
    partial_value = jnp.stack(pieces, axis=1).reshape(out_chan, taps) * (1.0 / math.sqrt(pixels))
    core_sum = halve_sum(partial_value, "row", core_bit, 1)
    col_sum = scatter_sum(core_sum, "col")
    row_piece = double_sum(col_sum, "row", [1 << 1, 3 << 1, 1 << 3, 3 << 3])
    own_share = double_join(row_piece, "row", core_bit, 1)
    weight_grad = own_share.T.reshape(3, 3, in_chan, share)
    features = outputs.reshape(img_count, tile_rows, tile_cols, out_chan)
    input_grad = grad_input.astype(jnp.bfloat16).reshape(img_count, tile_rows, tile_cols, in_chan)
    return (features, input_grad, weight_grad)


def solution(mesh):
    placed = (
        P("row", "col", None, None),
        P(None, None, None, "col"),
        P(),
        P("row", "col", None, None),
    )
    return jax.shard_map(
        on_device,
        mesh=mesh,
        in_specs=placed,
        out_specs=(
            P("row", "col", None, None),
            P("row", "col", None, None),
            P(None, None, None, "col"),
        ),
        check_vma=False,
    )
```

```python
import math

import jax
import jax.numpy as jnp
from jax import lax
from jax.sharding import PartitionSpec as P

epsilon = 1e-06
root_half = 0.7071067811865476
norm_const = 0.3989422804014327


def padded_2(value, sides, width):
    for axis, dim in sides:
        peers, length = (lax.axis_size(axis), value.shape[dim])
        up = [(i, (i + 1) % peers) for i in range(peers - 1)]
        down = [(j, i) for i, j in up]
        last = lax.slice_in_dim(value, length - width, length, axis=dim)
        initial = lax.slice_in_dim(value, 0, width, axis=dim)
        before = lax.ppermute(last, axis, up)
        after = lax.ppermute(initial, axis, down)
        value = jnp.concatenate([before, value, after], axis=dim)
    return value


def exchange(value, axis, bit, mask=None):
    peers = lax.axis_size(axis)
    mask = 1 << bit if mask is None else mask
    pairs = [(i, i ^ mask) for i in range(peers)]
    return lax.ppermute(value, axis, pairs)


def gather_chunks(value, axis):
    peers = lax.axis_size(axis)
    copies = jnp.broadcast_to(value[None], (peers,) + value.shape)
    return lax.all_to_all(copies, axis, 0, 0, tiled=False)


def scatter_sum(value, axis):
    peers = lax.axis_size(axis)
    blocks = value.reshape((peers, value.shape[0] // peers) + value.shape[1:])
    return lax.all_to_all(blocks, axis, 0, 0, tiled=False).sum(0)


def split_pair(value, upper, dim):
    low, high = jnp.split(value, 2, axis=dim)
    return jnp.where(upper, high, low), jnp.where(upper, low, high)


def join_pair(value, other, upper, dim):
    return jnp.where(upper, jnp.concatenate([other, value], dim), jnp.concatenate([value, other], dim))


def halve_sum(value, axis, bits, dim):
    me = lax.axis_index(axis)
    for bit in bits:
        keep, send = split_pair(value, ((me >> bit) & 1) == 1, dim)
        value = keep + exchange(send, axis, bit)
    return value


def double_sum(value, axis, masks):
    for mask in masks:
        value = value + exchange(value, axis, 0, mask)
    return value


def double_join(value, axis, bits, dim):
    me = lax.axis_index(axis)
    for bit in bits:
        value = join_pair(value, exchange(value, axis, bit), ((me >> bit) & 1) == 1, dim)
    return value


def norm_act(conv_out, upper, norm_gain):
    mean_val = jnp.mean(conv_out, axis=-1, keepdims=True)
    centred = conv_out - mean_val
    variance = jnp.mean(centred * centred, axis=-1, keepdims=True)
    inv_std = lax.rsqrt(variance + epsilon)
    unit = centred * inv_std
    normed = unit * norm_gain
    cdf_val = 0.5 * (1.0 + lax.erf(normed * root_half))
    density = jnp.exp(-0.5 * normed * normed) * norm_const
    outputs = (normed * cdf_val).astype(jnp.bfloat16)
    upstream = upper.astype(jnp.float32) * (cdf_val + normed * density) * norm_gain
    mean_up = jnp.mean(upstream, axis=-1, keepdims=True)
    mean_cross = jnp.mean(upstream * unit, axis=-1, keepdims=True)
    grad_pre = inv_std * (upstream - mean_up - unit * mean_cross)
    return (outputs, grad_pre.astype(jnp.bfloat16))


def window(padded, tap_row, tap_col, tile_rows, tile_cols):
    return padded[:, tap_row : tap_row + tile_rows, tap_col : tap_col + tile_cols, :].reshape(
        -1, padded.shape[-1]
    )


def on_device(images, weight, norm_gain, cotangent):
    img_count, tile_rows, tile_cols, in_chan = images.shape
    taps, share = 9 * in_chan, weight.shape[3]
    local_t = weight.reshape(taps, share).T
    core_bit = [0]
    half_t, _ = split_pair(local_t, (lax.axis_index("row") & 1) == 1, 1)
    kernel_t = double_join(gather_chunks(half_t, "col"), "row", core_bit, 2).reshape(-1, taps)
    out_chan = kernel_t.shape[0]
    whole_kernel = kernel_t.T.reshape(3, 3, in_chan, out_chan)
    both = jnp.concatenate([images, cotangent], axis=-1)
    rimmed = padded_2(both, (("col", 1),), 2)
    padded_all = jnp.pad(rimmed[..., :in_chan], ((0, 0), (0, 0), (1, 1), (0, 0)))
    rows = tile_rows + 2
    conv_out = jnp.zeros((img_count * rows * tile_cols, out_chan), jnp.float32)
    for tap_row in range(3):
        for tap_col in range(3):
            conv_out = conv_out + jnp.dot(
                window(padded_all, tap_row, tap_col, rows, tile_cols),
                whole_kernel[tap_row, tap_col],
                preferred_element_type=jnp.float32,
            )
    upper_cot = rimmed[:, 1 : rows + 1, :, in_chan:].reshape(-1, out_chan)
    outputs, grad_all = norm_act(conv_out, upper_cot, norm_gain)
    outputs = outputs.reshape(img_count, rows, tile_cols, out_chan)[:, 1 : tile_rows + 1]
    grad_all = grad_all.reshape(img_count, rows, tile_cols, out_chan)
    me, peers = lax.axis_index("col"), lax.axis_size("col")
    grid_row = jnp.arange(rows).reshape(1, rows, 1, 1)
    inside = ((grid_row > 0) | (me > 0)) & ((grid_row < rows - 1) | (me < peers - 1))
    grad_all = jnp.where(inside, grad_all, jnp.zeros_like(grad_all))
    grad_pad = jnp.pad(grad_all, ((0, 0), (0, 0), (1, 1), (0, 0)))
    grad_pre = grad_all[:, 1 : tile_rows + 1].reshape(-1, out_chan)
    padded = padded_all[:, 1 : rows + 1]
    grad_input = jnp.zeros((img_count * tile_rows * tile_cols, in_chan), jnp.float32)
    pieces = []
    for tap_row in range(3):
        for tap_col in range(3):
            grad_input = grad_input + lax.dot_general(
                window(grad_pad, 2 - tap_row, 2 - tap_col, tile_rows, tile_cols),
                whole_kernel[tap_row, tap_col],
                (((1,), (1,)), ((), ())),
                preferred_element_type=jnp.float32,
            )
            pieces.append(
                lax.dot_general(
                    grad_pre,
                    window(padded, tap_row, tap_col, tile_rows, tile_cols),
                    (((0,), (0,)), ((), ())),
                    preferred_element_type=jnp.float32,
                )
            )
    partial_value = jnp.stack(pieces, axis=1).reshape(out_chan, taps)
    core_sum = halve_sum(partial_value, "row", core_bit, 1)
    col_sum = scatter_sum(core_sum, "col")
    row_piece = double_sum(col_sum, "row", [1 << 1, 3 << 1, 1 << 3, 3 << 3])
    own_share = double_join(row_piece, "row", core_bit, 1)
    pixels = img_count * lax.axis_size("row") * tile_rows * lax.axis_size("col") * tile_cols
    weight_grad = (own_share * (1.0 / math.sqrt(pixels))).T.reshape(3, 3, in_chan, share)
    features = outputs
    input_grad = grad_input.astype(jnp.bfloat16).reshape(img_count, tile_rows, tile_cols, in_chan)
    return (features, input_grad, weight_grad)


def solution(mesh):
    placed = (
        P("row", "col", None, None),
        P(None, None, None, "col"),
        P(),
        P("row", "col", None, None),
    )
    return jax.shard_map(
        on_device,
        mesh=mesh,
        in_specs=placed,
        out_specs=(
            P("row", "col", None, None),
            P("row", "col", None, None),
            P(None, None, None, "col"),
        ),
        check_vma=False,
    )
```

```python
import math

import jax
import jax.numpy as jnp
from jax import lax
from jax.sharding import PartitionSpec as P

epsilon = 1e-06
root_half = 0.7071067811865476
norm_const = 0.3989422804014327


def padded_2(value, sides, width):
    for axis, dim in sides:
        peers, length = (lax.axis_size(axis), value.shape[dim])
        up = [(i, (i + 1) % peers) for i in range(peers - 1)]
        down = [(j, i) for i, j in up]
        last = lax.slice_in_dim(value, length - width, length, axis=dim)
        initial = lax.slice_in_dim(value, 0, width, axis=dim)
        before = lax.ppermute(last, axis, up)
        after = lax.ppermute(initial, axis, down)
        value = jnp.concatenate([before, value, after], axis=dim)
    return value


def exchange(value, axis, bit, mask=None):
    peers = lax.axis_size(axis)
    mask = 1 << bit if mask is None else mask
    pairs = [(i, i ^ mask) for i in range(peers)]
    return lax.ppermute(value, axis, pairs)


def gather_chunks(value, axis):
    peers = lax.axis_size(axis)
    copies = jnp.broadcast_to(value[None], (peers,) + value.shape)
    return lax.all_to_all(copies, axis, 0, 0, tiled=False)


def scatter_sum(value, axis):
    peers = lax.axis_size(axis)
    blocks = value.reshape((peers, value.shape[0] // peers) + value.shape[1:])
    return lax.all_to_all(blocks, axis, 0, 0, tiled=False).sum(0)


def split_pair(value, upper, dim):
    half = value.shape[dim] // 2
    at = upper.astype(jnp.int32) * half
    return lax.dynamic_slice_in_dim(value, at, half, dim), lax.dynamic_slice_in_dim(value, half - at, half, dim)


def join_pair(value, other, upper, dim):
    return jnp.where(upper, jnp.concatenate([other, value], dim), jnp.concatenate([value, other], dim))


def halve_sum(value, axis, bits, dim):
    me = lax.axis_index(axis)
    for bit in bits:
        keep, send = split_pair(value, ((me >> bit) & 1) == 1, dim)
        value = keep + exchange(send, axis, bit)
    return value


def double_sum(value, axis, masks):
    for mask in masks:
        value = value + exchange(value, axis, 0, mask)
    return value


def double_join(value, axis, bits, dim):
    me = lax.axis_index(axis)
    for bit in bits:
        value = join_pair(value, exchange(value, axis, bit), ((me >> bit) & 1) == 1, dim)
    return value


def norm_act(conv_out, upper, norm_gain):
    mean_val = jnp.mean(conv_out, axis=-1, keepdims=True)
    centred = conv_out - mean_val
    variance = jnp.mean(centred * centred, axis=-1, keepdims=True)
    inv_std = lax.rsqrt(variance + epsilon)
    unit = centred * inv_std
    normed = unit * norm_gain
    cdf_val = 0.5 * (1.0 + lax.erf(normed * root_half))
    density = jnp.exp(-0.5 * normed * normed) * norm_const
    outputs = (normed * cdf_val).astype(jnp.bfloat16)
    upstream = upper.astype(jnp.float32) * (cdf_val + normed * density) * norm_gain
    mean_up = jnp.mean(upstream, axis=-1, keepdims=True)
    mean_cross = jnp.mean(upstream * unit, axis=-1, keepdims=True)
    grad_pre = inv_std * (upstream - mean_up - unit * mean_cross)
    return (outputs, grad_pre.astype(jnp.bfloat16))


def window(padded, tap_row, tap_col, tile_rows, tile_cols):
    return padded[:, tap_row : tap_row + tile_rows, tap_col : tap_col + tile_cols, :].reshape(
        -1, padded.shape[-1]
    )


def on_device(images, weight, norm_gain, cotangent):
    img_count, tile_rows, tile_cols, in_chan = images.shape
    taps, share = 9 * in_chan, weight.shape[3]
    local_t = weight.reshape(taps, share).T
    core_bit = [0]
    half_t, _ = split_pair(local_t, (lax.axis_index("row") & 1) == 1, 1)
    kernel_t = double_join(gather_chunks(half_t, "col"), "row", core_bit, 2).reshape(-1, taps)
    out_chan = kernel_t.shape[0]
    whole_kernel = kernel_t.T.reshape(3, 3, in_chan, out_chan)
    rimmed = padded_2(images, (("col", 1),), 1)
    padded = jnp.pad(rimmed, ((0, 0), (0, 0), (1, 1), (0, 0)))
    conv_out = jnp.zeros((img_count * tile_rows * tile_cols, out_chan), jnp.float32)
    for tap_row in range(3):
        for tap_col in range(3):
            conv_out = conv_out + jnp.dot(
                window(padded, tap_row, tap_col, tile_rows, tile_cols),
                whole_kernel[tap_row, tap_col],
                preferred_element_type=jnp.float32,
            )
    outputs, grad_pre = norm_act(conv_out, cotangent.reshape(-1, out_chan), norm_gain)
    grad_grid = grad_pre.reshape(img_count, tile_rows, tile_cols, out_chan)
    grad_rimmed = padded_2(grad_grid, (("col", 1),), 1)
    grad_pad = jnp.pad(grad_rimmed, ((0, 0), (0, 0), (1, 1), (0, 0)))
    grad_input = jnp.zeros((img_count * tile_rows * tile_cols, in_chan), jnp.float32)
    pieces = []
    for tap_row in range(3):
        for tap_col in range(3):
            grad_input = grad_input + lax.dot_general(
                window(grad_pad, 2 - tap_row, 2 - tap_col, tile_rows, tile_cols),
                whole_kernel[tap_row, tap_col],
                (((1,), (1,)), ((), ())),
                preferred_element_type=jnp.float32,
            )
            pieces.append(
                lax.dot_general(
                    grad_pre,
                    window(padded, tap_row, tap_col, tile_rows, tile_cols),
                    (((0,), (0,)), ((), ())),
                    preferred_element_type=jnp.float32,
                )
            )
    partial_value = jnp.stack(pieces, axis=1).reshape(out_chan, taps)
    core_sum = halve_sum(partial_value, "row", core_bit, 1)
    col_sum = scatter_sum(core_sum, "col")
    row_piece = double_sum(col_sum, "row", [1 << 1, 3 << 1, 1 << 3, 3 << 3])
    own_share = double_join(row_piece, "row", core_bit, 1)
    pixels = img_count * lax.axis_size("row") * tile_rows * lax.axis_size("col") * tile_cols
    weight_grad = (own_share * (1.0 / math.sqrt(pixels))).T.reshape(3, 3, in_chan, share)
    features = outputs.reshape(img_count, tile_rows, tile_cols, out_chan)
    input_grad = grad_input.astype(jnp.bfloat16).reshape(img_count, tile_rows, tile_cols, in_chan)
    return (features, input_grad, weight_grad)


def solution(mesh):
    placed = (
        P("row", "col", None, None),
        P(None, None, None, "col"),
        P(),
        P("row", "col", None, None),
    )
    return jax.shard_map(
        on_device,
        mesh=mesh,
        in_specs=placed,
        out_specs=(
            P("row", "col", None, None),
            P("row", "col", None, None),
            P(None, None, None, "col"),
        ),
        check_vma=False,
    )
```

```python
import math

import jax
import jax.numpy as jnp
from jax import lax
from jax.sharding import PartitionSpec as P

epsilon = 1e-06
root_half = 0.7071067811865476
norm_const = 0.3989422804014327


def padded_2(value, sides, width):
    for axis, dim in sides:
        peers, length = (lax.axis_size(axis), value.shape[dim])
        up = [(i, (i + 1) % peers) for i in range(peers - 1)]
        down = [(j, i) for i, j in up]
        last = lax.slice_in_dim(value, length - width, length, axis=dim)
        initial = lax.slice_in_dim(value, 0, width, axis=dim)
        before = lax.ppermute(last, axis, up)
        after = lax.ppermute(initial, axis, down)
        value = jnp.concatenate([before, value, after], axis=dim)
    return value


def exchange(value, axis, bit, mask=None):
    peers = lax.axis_size(axis)
    mask = 1 << bit if mask is None else mask
    pairs = [(i, i ^ mask) for i in range(peers)]
    return lax.ppermute(value, axis, pairs)


def gather_chunks(value, axis):
    peers = lax.axis_size(axis)
    copies = jnp.broadcast_to(value[None], (peers,) + value.shape)
    return lax.all_to_all(copies, axis, 0, 0, tiled=False)


def scatter_sum(value, axis):
    peers = lax.axis_size(axis)
    blocks = value.reshape((peers, value.shape[0] // peers) + value.shape[1:])
    return lax.all_to_all(blocks, axis, 0, 0, tiled=False).sum(0)


def split_pair(value, upper, dim):
    low, high = jnp.split(value, 2, axis=dim)
    return jnp.where(upper, high, low), jnp.where(upper, low, high)


def join_pair(value, other, upper, dim):
    return jnp.where(upper, jnp.concatenate([other, value], dim), jnp.concatenate([value, other], dim))


def halve_sum(value, axis, bits, dim):
    me = lax.axis_index(axis)
    for bit in bits:
        half = value.shape[dim] // 2
        at = ((me >> bit) & 1) * half
        keep = lax.dynamic_slice_in_dim(value, at, half, dim)
        send = lax.dynamic_slice_in_dim(value, half - at, half, dim)
        value = keep + exchange(send, axis, bit)
    return value


def double_sum(value, axis, masks):
    for mask in masks:
        value = value + exchange(value, axis, 0, mask)
    return value


def double_join(value, axis, bits, dim):
    me = lax.axis_index(axis)
    for bit in bits:
        value = join_pair(value, exchange(value, axis, bit), ((me >> bit) & 1) == 1, dim)
    return value


def norm_act(conv_out, upper, norm_gain):
    mean_val = jnp.mean(conv_out, axis=-1, keepdims=True)
    centred = conv_out - mean_val
    variance = jnp.mean(centred * centred, axis=-1, keepdims=True)
    inv_std = lax.rsqrt(variance + epsilon)
    unit = centred * inv_std
    normed = unit * norm_gain
    cdf_val = 0.5 * (1.0 + lax.erf(normed * root_half))
    density = jnp.exp(-0.5 * normed * normed) * norm_const
    outputs = (normed * cdf_val).astype(jnp.bfloat16)
    upstream = upper.astype(jnp.float32) * (cdf_val + normed * density) * norm_gain
    mean_up = jnp.mean(upstream, axis=-1, keepdims=True)
    mean_cross = jnp.mean(upstream * unit, axis=-1, keepdims=True)
    grad_pre = inv_std * (upstream - mean_up - unit * mean_cross)
    return (outputs, grad_pre.astype(jnp.bfloat16))


def window(padded, tap_row, tap_col, tile_rows, tile_cols):
    return padded[:, tap_row : tap_row + tile_rows, tap_col : tap_col + tile_cols, :].reshape(
        -1, padded.shape[-1]
    )


def on_device(images, weight, norm_gain, cotangent):
    img_count, tile_rows, tile_cols, in_chan = images.shape
    taps, share = 9 * in_chan, weight.shape[3]
    local_t = weight.reshape(taps, share).T
    core_bit = [0]
    half_t, _ = split_pair(local_t, (lax.axis_index("row") & 1) == 1, 1)
    kernel_t = double_join(gather_chunks(half_t, "col"), "row", core_bit, 2).reshape(-1, taps)
    out_chan = kernel_t.shape[0]
    whole_kernel = kernel_t.T.reshape(3, 3, in_chan, out_chan)
    rimmed = padded_2(images, (("col", 1),), 1)
    padded = jnp.pad(rimmed, ((0, 0), (0, 0), (1, 1), (0, 0)))
    conv_out = jnp.zeros((img_count * tile_rows * tile_cols, out_chan), jnp.float32)
    for tap_row in range(3):
        for tap_col in range(3):
            conv_out = conv_out + jnp.dot(
                window(padded, tap_row, tap_col, tile_rows, tile_cols),
                whole_kernel[tap_row, tap_col],
                preferred_element_type=jnp.float32,
            )
    outputs, grad_pre = norm_act(conv_out, cotangent.reshape(-1, out_chan), norm_gain)
    grad_grid = grad_pre.reshape(img_count, tile_rows, tile_cols, out_chan)
    grad_rimmed = padded_2(grad_grid, (("col", 1),), 1)
    grad_pad = jnp.pad(grad_rimmed, ((0, 0), (0, 0), (1, 1), (0, 0)))
    grad_input = jnp.zeros((img_count * tile_rows * tile_cols, in_chan), jnp.float32)
    pieces = []
    for tap_row in range(3):
        for tap_col in range(3):
            grad_input = grad_input + lax.dot_general(
                window(grad_pad, 2 - tap_row, 2 - tap_col, tile_rows, tile_cols),
                whole_kernel[tap_row, tap_col],
                (((1,), (1,)), ((), ())),
                preferred_element_type=jnp.float32,
            )
            pieces.append(
                lax.dot_general(
                    grad_pre,
                    window(padded, tap_row, tap_col, tile_rows, tile_cols),
                    (((0,), (0,)), ((), ())),
                    preferred_element_type=jnp.float32,
                )
            )
    partial_value = jnp.stack(pieces, axis=1).reshape(out_chan, taps)
    core_sum = halve_sum(partial_value, "row", core_bit, 1)
    col_sum = scatter_sum(core_sum, "col")
    row_piece = double_sum(col_sum, "row", [1 << 1, 3 << 1, 1 << 3, 3 << 3])
    own_share = double_join(row_piece, "row", core_bit, 1)
    pixels = img_count * lax.axis_size("row") * tile_rows * lax.axis_size("col") * tile_cols
    weight_grad = (own_share * (1.0 / math.sqrt(pixels))).T.reshape(3, 3, in_chan, share)
    features = outputs.reshape(img_count, tile_rows, tile_cols, out_chan)
    input_grad = grad_input.astype(jnp.bfloat16).reshape(img_count, tile_rows, tile_cols, in_chan)
    return (features, input_grad, weight_grad)


def solution(mesh):
    placed = (
        P("row", "col", None, None),
        P(None, None, None, "col"),
        P(),
        P("row", "col", None, None),
    )
    return jax.shard_map(
        on_device,
        mesh=mesh,
        in_specs=placed,
        out_specs=(
            P("row", "col", None, None),
            P("row", "col", None, None),
            P(None, None, None, "col"),
        ),
        check_vma=False,
    )
```
